256 devices in a mesh: dp: 64 (over z, y_lo, x), mp: 4 (over y_hi, core).
Axes of the slice: x: 4, y: 4 (y_hi: 2, y_lo: 2; y = y_hi * 2 + y_lo), z: 8, core: 2. Of those that a mesh axis runs over, the one named last changes fastest.
Arguments:
- tokens: bfloat16 [16384, 2048], P(('dp', 'mp')), may hold values from -6 to 6
- attn_gain: float32 [2048], replicated, may hold values from 0.1 to 1.9
- query_weight: float32 [2048, 1280], P('dp', 'mp'), may hold values from -0.125 to 0.125
- key_value_weight: float32 [2048, 640], P(('dp', 'mp')), may hold values from -0.125 to 0.125
- query_gain: float32 [64], replicated, may hold values from 0.6 to 7
- key_gain: float32 [64], replicated, may hold values from 0.6 to 7
- out_weight: float32 [1280, 2048], P('mp', 'dp'), may hold values from -0.15625 to 0.15625
- ffn_gain: float32 [2048], replicated, may hold values from 0.1 to 1.9
- gate_up_weight: float32 [2, 2048, 5120], P(None, 'dp', 'mp'), may hold values from -0.125 to 0.125
- down_weight: float32 [5120, 2048], P('mp', 'dp'), may hold values from -0.078125 to 0.078125
- prompt_lengths: int32 [64, 2], P('dp'), may hold values from 1 to 192, 256 in all within a row
- page_table: int32 [1024], P('dp'), may hold values from 0 to 1023, as said below
Outputs:
- layer_out: bfloat16 [16384, 2048], P(('dp', 'mp'))
- kv_pool: bfloat16 [1024, 16, 640], P('dp')
The draws below stay inside these ranges and needn't reach their ends.
Inputs may be any that keep to these rules, and one draw needn't show every extreme that they name: `prompt_lengths`: each row sums to 256. `page_table`: a permutation of the pool slots; slot q lies on the index q // 16 of dp; at most 1 pages of one index of dp have slots on one owner.
All inputs are finite; a program needn't handle non-finite values.
Results may differ from the reference program's by a relative error of at most 0.02.
The reference program's roundings to bfloat16 on the way count: a program that leaves them out, or rounds other values in their place, can miss the bound.
Values may be sent and summed in bfloat16 or wider, within the bound.
No kernel may reach another device: no remote copies, remote signals or barrier semaphores. Data moves between devices by JAX's collectives and lax.ppermute only.
A program may use at most 64 MiB of HBM per device.

```python
import math
import jax
import jax.numpy as jnp
import numpy as np
from jax import lax

MODEL_WIDTH = 2048
QUERY_HEADS = 20
KEYVALUE_HEADS = 5
HEAD_SIZE = 64
FF = 5120
PAGE_SLOTS = 16
SEQ_DEV = 2
TOKENS_PER_SHARD = 256
MAXLEN = 192
GROUPS = 64
TOKENS = 16384
PAGES_DEV = 16
TOTAL_PAGES = 1024
CAP = 1


def head_gain(key):
    return jnp.exp(jax.random.uniform(key, (HEAD_SIZE,), jnp.float32, -0.5, 0.5))


def draw_query_gain(key, part):
    return head_gain(jax.random.fold_in(key, 17))


def draw_key_gain(key, part):
    return head_gain(jax.random.fold_in(key, 29))


def draw_page_table(key, part):
    owners = min(PAGES_DEV, GROUPS)
    shuffle = jax.random.permutation(jax.random.fold_in(key, 41), GROUPS).astype(jnp.int32)
    offsets = jax.random.permutation(jax.random.fold_in(key, 43), GROUPS).astype(jnp.int32)[:owners]
    page_ids = jnp.arange(TOTAL_PAGES, dtype=jnp.int32)
    sender = page_ids // PAGES_DEV
    within = page_ids % PAGES_DEV
    column = within // CAP
    owner = shuffle[(sender + offsets[column]) % GROUPS]
    return (owner * PAGES_DEV + column * CAP + within % CAP).astype(jnp.int32)


def block_scale(rng, dims, shards, smallest, largest):
    factor_of, own = 1.0, jax.random.fold_in(rng, 6)
    for dim, shards_of in shards:
        draws = jnp.exp(jax.random.uniform(jax.random.fold_in(own, dim), (shards_of,), jnp.float32, smallest / len(shards), largest / len(shards)))
        factor_of = factor_of * jnp.repeat(draws, dims[dim] // shards_of).reshape([-1 if axis == dim else 1 for axis in range(len(dims))])
    return factor_of


def length_profile(number_of, total, most, lean):
    portions = [(1 << 20) // math.isqrt(grade ** lean) + 1 for grade in range(2, number_of + 1)]
    rest, given = total - most - (number_of - 1), [1] * (number_of - 1)
    while rest > 0:
        candidates = [i for i in range(number_of - 1) if given[i] < most]
        mass, left = sum([portions[i] for i in candidates]), rest
        for i in candidates:
            addition = min(most - given[i], max(1, left * portions[i] // mass), rest)
            given[i] = given[i] + addition
            rest = rest - addition
    return np.array([most] + given)


def ragged_sizes(key, number_of, total, most, skew):
    if number_of == 2:
        one = jax.random.randint(key, (), max(1, total - most), min(most, total - 1) + 1)
        return jnp.stack([one, total - one])
    sizes = jnp.asarray(length_profile(number_of, total, most, skew), jnp.int32)
    couples = (number_of - 1) // 2
    donor, receiver = sizes[1:1 + 2 * couples:2], sizes[2:2 + 2 * couples:2]
    slack = jnp.minimum(donor - 1, most - receiver)
    moved = jax.random.randint(jax.random.fold_in(key, 1), (couples,), 0, 1 << 20) % (slack + 1)
    sizes = sizes.at[1:1 + 2 * couples:2].set(donor - moved).at[2:2 + 2 * couples:2].set(receiver + moved)
    return sizes[jax.random.permutation(jax.random.fold_in(key, 2), number_of)]


def gaussian(own_key, extent, deviation, most, pieces=(), kind=jnp.bfloat16):
    array = deviation * jax.random.normal(own_key, extent, jnp.float32)
    if pieces:
        array = array * block_scale(own_key, extent, pieces, -0.22, 0.18)
    return jnp.clip(array, -most, most).astype(kind)


def setup_inputs(seed: int = 0) -> dict:
    arg_keys = jax.random.split(jax.random.key(seed), 13)
    tokens = gaussian(arg_keys[0], (TOKENS, MODEL_WIDTH), 1.0, 6.0, ((0, 256),))
    attn_gain = jnp.clip(1.0 + 0.18 * jax.random.normal(arg_keys[1], (MODEL_WIDTH,), jnp.float32), 0.1, 1.9)
    query_weight = gaussian(arg_keys[2], (MODEL_WIDTH, QUERY_HEADS * HEAD_SIZE), MODEL_WIDTH ** -0.5, 0.125, ((0, 64), (1, 4)), jnp.float32)
    key_value_weight = gaussian(arg_keys[3], (MODEL_WIDTH, 2 * KEYVALUE_HEADS * HEAD_SIZE), MODEL_WIDTH ** -0.5, 0.125, ((0, 256),), jnp.float32)
    query_gain = draw_query_gain(jax.random.fold_in(arg_keys[12], 71), 0)
    key_gain = draw_key_gain(jax.random.fold_in(arg_keys[12], 71), 0)
    out_weight = gaussian(arg_keys[6], (QUERY_HEADS * HEAD_SIZE, MODEL_WIDTH), (QUERY_HEADS * HEAD_SIZE) ** -0.5, 0.15625, ((0, 4), (1, 64)), jnp.float32)
    ffn_gain = jnp.clip(1.0 + 0.18 * jax.random.normal(arg_keys[7], (MODEL_WIDTH,), jnp.float32), 0.1, 1.9)
    gate_up_weight = gaussian(arg_keys[8], (2, MODEL_WIDTH, FF), MODEL_WIDTH ** -0.5, 0.125, ((1, 64), (2, 4)), jnp.float32)
    down_weight = gaussian(arg_keys[9], (FF, MODEL_WIDTH), FF ** -0.5, 0.078125, ((0, 4), (1, 64)), jnp.float32)
    prompt_lengths = jax.vmap(lambda own: ragged_sizes(own, SEQ_DEV, TOKENS_PER_SHARD, MAXLEN, 2))(jax.random.split(arg_keys[10], GROUPS)).reshape((GROUPS, SEQ_DEV)).astype(jnp.int32)
    page_table = draw_page_table(jax.random.fold_in(arg_keys[12], 71), 0)
    return dict(tokens=tokens, attn_gain=attn_gain, query_weight=query_weight, key_value_weight=key_value_weight, query_gain=query_gain, key_gain=key_gain, out_weight=out_weight, ffn_gain=ffn_gain, gate_up_weight=gate_up_weight, down_weight=down_weight, prompt_lengths=prompt_lengths, page_table=page_table)


EPSILON = 1e-06

def rms_rows(values, gain):
    scale = lax.rsqrt(lax.optimization_barrier(jnp.mean(values * values, axis=-1, keepdims=True)) + EPSILON)
    return values * scale * gain

def prompt_layout(lengths, row_count, head_dim):
    ends = jnp.cumsum(lengths).astype(jnp.int32)
    starts = (ends - lengths).astype(jnp.int32)
    row_index = jnp.arange(row_count, dtype=jnp.int32)
    segment = lax.optimization_barrier(jnp.sum((row_index[:, None] >= ends[None, :]).astype(jnp.int32), axis=1)).astype(jnp.int32)
    prompt_ids = jnp.arange(lengths.shape[0], dtype=jnp.int32)
    first_row = lax.optimization_barrier(jnp.sum(jnp.where(segment[:, None] == prompt_ids[None, :], starts[None, :], 0), axis=1)).astype(jnp.int32)
    position = row_index - first_row
    half_dim = head_dim // 2
    frequency = 10000.0 ** (-(jnp.arange(half_dim, dtype=jnp.float32) * (2.0 / head_dim)))
    angle = position.astype(jnp.float32)[:, None] * frequency[None, :]
    allowed = (segment[:, None] == segment[None, :]) & (row_index[None, :] <= row_index[:, None])
    return (allowed, jnp.cos(angle)[:, None, :], jnp.sin(angle)[:, None, :])

def rotate_heads(flat, gain, cosines, sines):
    row_count = flat.shape[0]
    head_dim = gain.shape[0]
    heads = rms_rows(flat.reshape(row_count, -1, head_dim), gain)
    half_dim = head_dim // 2
    first = heads[..., :half_dim]
    second = heads[..., half_dim:]
    turned = jnp.concatenate([first * cosines - second * sines, second * cosines + first * sines], axis=-1)
    return turned.reshape(row_count, -1)

def softmax_rows(scores):
    peak = lax.optimization_barrier(jnp.max(scores, axis=-1, keepdims=True))
    weights = jnp.exp(scores - peak)
    return weights / lax.optimization_barrier(jnp.sum(weights, axis=-1, keepdims=True))

def reference(tokens, attn_gain, query_weight, key_value_weight, query_gain, key_gain, out_weight, ffn_gain, gate_up_weight, down_weight, prompt_lengths, page_table):
    query_server = query_weight.astype(jnp.bfloat16)
    keyval_server = key_value_weight.astype(jnp.bfloat16)
    out_server = out_weight.astype(jnp.bfloat16)
    gate_up_server = gate_up_weight.astype(jnp.bfloat16)
    down_server = down_weight.astype(jnp.bfloat16)
    key_column_width = KEYVALUE_HEADS * HEAD_SIZE
    shard_portion = QUERY_HEADS // KEYVALUE_HEADS

    def one_group(operands):
        group_tokens, lengths = operands
        inputs_wide = group_tokens.astype(jnp.float32)
        normed = rms_rows(inputs_wide, attn_gain).astype(jnp.bfloat16)
        queries = jnp.dot(normed, query_server, preferred_element_type=jnp.float32)
        keyvals = jnp.dot(normed, keyval_server, preferred_element_type=jnp.float32)
        allowed, cosines, sines = prompt_layout(lengths, TOKENS_PER_SHARD, HEAD_SIZE)
        query_heads = rotate_heads(queries, query_gain, cosines, sines).astype(jnp.bfloat16)
        key_head_rows = rotate_heads(keyvals[:, :key_column_width], key_gain, cosines, sines).astype(jnp.bfloat16)
        value_head_rows = keyvals[:, key_column_width:].astype(jnp.bfloat16)
        query_grid = query_heads.reshape(TOKENS_PER_SHARD, QUERY_HEADS, HEAD_SIZE).astype(jnp.float32)
        key_page_grid = jnp.repeat(key_head_rows.reshape(TOKENS_PER_SHARD, KEYVALUE_HEADS, HEAD_SIZE), shard_portion, axis=1).astype(jnp.float32)
        value_page_grid = jnp.repeat(value_head_rows.reshape(TOKENS_PER_SHARD, KEYVALUE_HEADS, HEAD_SIZE), shard_portion, axis=1).astype(jnp.float32)
        scores = jnp.einsum('qhd,khd->hqk', query_grid, key_page_grid) * HEAD_SIZE ** (-0.5)
        scores = jnp.where(allowed[None, :, :], scores, -1e+30)
        probs = softmax_rows(scores).astype(jnp.bfloat16)
        attended = jnp.einsum('hqk,khd->qhd', probs.astype(jnp.float32), value_page_grid)
        attended = attended.astype(jnp.bfloat16).reshape(TOKENS_PER_SHARD, QUERY_HEADS * HEAD_SIZE)
        residual = inputs_wide + jnp.dot(attended, out_server, preferred_element_type=jnp.float32)
        ffn_input = rms_rows(residual, ffn_gain).astype(jnp.bfloat16)
        gate = jnp.dot(ffn_input, gate_up_server[0], preferred_element_type=jnp.float32)
        upward = jnp.dot(ffn_input, gate_up_server[1], preferred_element_type=jnp.float32)
        hidden = (jax.nn.silu(gate) * upward).astype(jnp.bfloat16)
        result_rows = (residual + jnp.dot(hidden, down_server, preferred_element_type=jnp.float32)).astype(jnp.bfloat16)
        cache_rows = jnp.concatenate([key_head_rows, value_head_rows], axis=1)
        return (result_rows, cache_rows)
    grouped = tokens.reshape(GROUPS, TOKENS_PER_SHARD, MODEL_WIDTH)
    result_groups, cache_head_groups = lax.map(one_group, (grouped, prompt_lengths))
    cache_pages = cache_head_groups.reshape(TOTAL_PAGES, PAGE_SLOTS, 2 * KEYVALUE_HEADS * HEAD_SIZE)
    kv_pool = jnp.zeros_like(cache_pages).at[page_table].set(cache_pages)
    layer_out = result_groups.reshape(TOKENS, MODEL_WIDTH)
    return (layer_out, kv_pool)
```

```python
import jax
import jax.numpy as jnp
from jax import lax
from jax.sharding import Mesh, PartitionSpec as P

QUERY_HEADS = 20
KEYVALUE_HEADS = 5
PAGE_SLOTS = 16


EPSILON = 1e-06


def rms_rows(values, gain):
    scale = lax.rsqrt(jnp.mean(values * values, axis=-1, keepdims=True) + EPSILON)
    return values * scale * gain


def prompt_layout(lengths, row_count, head_dim):
    ends = jnp.cumsum(lengths)
    starts = ends - lengths
    row_index = jnp.arange(row_count, dtype=jnp.int32)
    segment = jnp.sum((row_index[:, None] >= ends[None, :]).astype(jnp.int32), axis=1)
    prompt_ids = jnp.arange(lengths.shape[0], dtype=jnp.int32)
    first_row = jnp.sum(
        jnp.where(segment[:, None] == prompt_ids[None, :], starts[None, :], 0), axis=1
    )
    position = row_index - first_row
    half_dim = head_dim // 2
    frequency = 10000.0 ** (-(jnp.arange(half_dim, dtype=jnp.float32) * (2.0 / head_dim)))
    angle = position.astype(jnp.float32)[:, None] * frequency[None, :]
    allowed = (segment[:, None] == segment[None, :]) & (row_index[None, :] <= row_index[:, None])
    return (allowed, jnp.cos(angle)[:, None, :], jnp.sin(angle)[:, None, :])


def rotate_heads(flat, gain, cosines, sines):
    row_count = flat.shape[0]
    head_dim = gain.shape[0]
    heads = rms_rows(flat.reshape(row_count, -1, head_dim), gain)
    half_dim = head_dim // 2
    first = heads[..., :half_dim]
    second = heads[..., half_dim:]
    turned = jnp.concatenate(
        [first * cosines - second * sines, second * cosines + first * sines], axis=-1
    )
    return turned.reshape(row_count, -1)


def softmax_rows(scores):
    peak = jnp.max(scores, axis=-1, keepdims=True)
    weights = jnp.exp(scores - peak)
    return weights / jnp.sum(weights, axis=-1, keepdims=True)


def fold_rows(left, piece):
    return jnp.dot(left, piece, preferred_element_type=jnp.float32)


DP_AXES = ("z", "ylo", "x")
MP_AXES = ("yhi", "core")


def gather_dp(flat):
    staged = flat[None]
    for axis in ("x", "ylo", "z"):
        staged = lax.all_gather(staged, axis, axis=0, tiled=True)
    return staged


def per_device(
    tokens,
    attn_gain,
    query_weight,
    key_value_weight,
    query_gain,
    key_gain,
    out_weight,
    ffn_gain,
    gate_up_weight,
    down_weight,
    prompt_lengths,
    page_table,
):
    head_dim = query_gain.shape[0]
    data_groups = 1
    for axis in DP_AXES:
        data_groups *= lax.axis_size(axis)
    part_index = lax.axis_index(MP_AXES)
    own_rows = tokens.shape[0]
    group_tokens = lax.all_gather(tokens, MP_AXES, axis=0, tiled=True)
    row_count = group_tokens.shape[0]
    inputs_wide = group_tokens.astype(jnp.float32)
    normed = rms_rows(inputs_wide, attn_gain).astype(jnp.bfloat16)
    model_width = tokens.shape[1]
    query_cols = query_weight.shape[1]
    keyval_cols = key_value_weight.shape[1]
    kv_rows = lax.all_gather(key_value_weight, MP_AXES, axis=0, tiled=True)
    pieces = [
        query_weight,
        kv_rows,
        out_weight,
        gate_up_weight,
        down_weight,
    ]
    sizes = [piece.size for piece in pieces]
    packed_weights = jnp.concatenate([piece.astype(jnp.bfloat16).reshape(-1) for piece in pieces])
    gathered = gather_dp(packed_weights)
    offsets = [0]
    for size in sizes:
        offsets.append(offsets[-1] + size)
    def piece_of(k):
        return gathered[:, offsets[k]:offsets[k + 1]]
    query_full = piece_of(0).reshape(model_width, query_cols)
    keyval_full = piece_of(1).reshape(model_width, keyval_cols)
    out_rows = out_weight.shape[0]
    out_grid = piece_of(2).reshape(data_groups, out_rows, out_weight.shape[1])
    gate_up_grid = piece_of(3).reshape((data_groups,) + gate_up_weight.shape)
    down_grid = piece_of(4).reshape((data_groups,) + down_weight.shape)
    queries = fold_rows(normed, query_full)
    keyvals = fold_rows(normed, keyval_full)
    allowed, cosines, sines = prompt_layout(prompt_lengths[0], row_count, head_dim)
    key_column_width = keyval_cols // 2
    query_heads = rotate_heads(queries, query_gain, cosines, sines).astype(jnp.bfloat16)
    key_head_rows = rotate_heads(keyvals[:, :key_column_width], key_gain, cosines, sines).astype(
        jnp.bfloat16
    )
    value_head_rows = keyvals[:, key_column_width:].astype(jnp.bfloat16)
    cache_rows = jnp.concatenate([key_head_rows, value_head_rows], axis=1)
    pages_here = row_count // PAGE_SLOTS
    cache_pages = cache_rows.reshape(pages_here, PAGE_SLOTS, keyval_cols)
    capacity = pages_here // min(pages_here, data_groups)
    owner = page_table // pages_here
    target = page_table % pages_here
    page_index = jnp.arange(pages_here, dtype=jnp.int32)
    earlier = (owner[None, :] == owner[:, None]) & (page_index[None, :] < page_index[:, None])
    send_slot = owner * capacity + jnp.sum(earlier.astype(jnp.int32), axis=1)
    slot_ids = jnp.arange(data_groups * capacity, dtype=jnp.int32)
    placing = slot_ids[:, None] == send_slot[None, :]
    send_marks = jnp.sum(jnp.where(placing, target[None, :] + 1, 0), axis=1).reshape(
        data_groups, capacity
    )
    flat_rows = cache_pages.reshape(pages_here, -1)
    packed = jnp.dot(placing.astype(jnp.bfloat16), flat_rows, preferred_element_type=jnp.float32)
    got_pages = lax.all_to_all(
        packed.astype(jnp.bfloat16).reshape(data_groups, capacity, -1),
        DP_AXES,
        split_axis=0,
        concat_axis=0,
        tiled=True,
    )
    got_marks = lax.all_to_all(send_marks, DP_AXES, split_axis=0, concat_axis=0, tiled=True)
    flat_rows = got_pages.reshape(data_groups * capacity, -1)
    choosing = (got_marks.reshape(-1)[None, :] == page_index[:, None] + 1).astype(jnp.bfloat16)
    kv_pool = (
        jnp.dot(choosing, flat_rows, preferred_element_type=jnp.float32)
        .astype(jnp.bfloat16)
        .reshape(pages_here, PAGE_SLOTS, keyval_cols)
    )
    heads_here = query_cols // head_dim
    shard_portion = QUERY_HEADS // KEYVALUE_HEADS
    kv_heads = key_column_width // head_dim
    global_heads = part_index * heads_here + jnp.arange(heads_here, dtype=jnp.int32)
    source_heads = global_heads // shard_portion
    query_grid = query_heads.reshape(row_count, heads_here, head_dim)
    key_page_grid = jnp.take(
        key_head_rows.reshape(row_count, kv_heads, head_dim), source_heads, axis=1
    )
    value_page_grid = jnp.take(
        value_head_rows.reshape(row_count, kv_heads, head_dim), source_heads, axis=1
    )
    scores = jnp.einsum(
        "qhd,khd->hqk", query_grid, key_page_grid, preferred_element_type=jnp.float32
    ) * head_dim ** (-0.5)
    scores = jnp.where(allowed[None, :, :], scores, -1e30)
    probs = softmax_rows(scores).astype(jnp.bfloat16)
    attended = jnp.einsum(
        "hqk,khd->qhd", probs, value_page_grid, preferred_element_type=jnp.float32
    )
    attended = attended.astype(jnp.bfloat16).reshape(row_count, query_cols)
    attn_part = jnp.einsum(
        "tr,grc->tgc", attended, out_grid, preferred_element_type=jnp.float32
    ).reshape(row_count, model_width)
    attn_total = lax.psum(attn_part.astype(jnp.bfloat16), MP_AXES).astype(jnp.float32)
    residual_all = inputs_wide + attn_total
    ffn_input = rms_rows(residual_all, ffn_gain).astype(jnp.bfloat16)
    residual_own = lax.dynamic_slice_in_dim(residual_all, part_index * own_rows, own_rows, 0)
    gate_up = jnp.einsum(
        "tgk,gskf->stf",
        ffn_input.reshape(row_count, data_groups, -1),
        gate_up_grid,
        preferred_element_type=jnp.float32,
    )
    hidden = (jax.nn.silu(gate_up[0]) * gate_up[1]).astype(jnp.bfloat16)
    down_part = jnp.einsum(
        "tf,gfc->tgc", hidden, down_grid, preferred_element_type=jnp.float32
    ).reshape(row_count, model_width)
    layer_out = (
        residual_own
        + lax.psum_scatter(
            down_part.astype(jnp.bfloat16),
            MP_AXES,
            scatter_dimension=0,
            tiled=True,
        ).astype(jnp.float32)
    ).astype(jnp.bfloat16)
    return (layer_out, kv_pool)


def solution(mesh):
    sizes = [mesh.shape["dp"] // (2 * 4), 2, 4, 2, mesh.shape["mp"] // 2]
    fine_mesh = Mesh(mesh.devices.reshape(sizes), DP_AXES + MP_AXES)
    rows = DP_AXES + MP_AXES
    return jax.shard_map(
        per_device,
        mesh=fine_mesh,
        in_specs=(
            P(rows, None),
            P(),
            P(DP_AXES, MP_AXES),
            P(rows, None),
            P(),
            P(),
            P(MP_AXES, DP_AXES),
            P(),
            P(None, DP_AXES, MP_AXES),
            P(MP_AXES, DP_AXES),
            P(DP_AXES, None),
            P(DP_AXES),
        ),
        out_specs=(P(rows, None), P(DP_AXES, None, None)),
        check_vma=False,
    )
```

```python
import jax
import jax.numpy as jnp
from jax import lax
from jax.sharding import Mesh, PartitionSpec as P

QUERY_HEADS = 20
KEYVALUE_HEADS = 5
PAGE_SLOTS = 16


EPSILON = 1e-06


def rms_rows(values, gain):
    scale = lax.rsqrt(jnp.mean(values * values, axis=-1, keepdims=True) + EPSILON)
    return values * scale * gain


def prompt_layout(lengths, row_count, head_dim):
    ends = jnp.cumsum(lengths)
    starts = ends - lengths
    row_index = jnp.arange(row_count, dtype=jnp.int32)
    segment = jnp.sum((row_index[:, None] >= ends[None, :]).astype(jnp.int32), axis=1)
    prompt_ids = jnp.arange(lengths.shape[0], dtype=jnp.int32)
    first_row = jnp.sum(
        jnp.where(segment[:, None] == prompt_ids[None, :], starts[None, :], 0), axis=1
    )
    position = row_index - first_row
    half_dim = head_dim // 2
    frequency = 10000.0 ** (-(jnp.arange(half_dim, dtype=jnp.float32) * (2.0 / head_dim)))
    angle = position.astype(jnp.float32)[:, None] * frequency[None, :]
    allowed = (segment[:, None] == segment[None, :]) & (row_index[None, :] <= row_index[:, None])
    return (allowed, jnp.cos(angle)[:, None, :], jnp.sin(angle)[:, None, :])


def rotate_heads(flat, gain, cosines, sines):
    row_count = flat.shape[0]
    head_dim = gain.shape[0]
    heads = rms_rows(flat.reshape(row_count, -1, head_dim), gain)
    half_dim = head_dim // 2
    first = heads[..., :half_dim]
    second = heads[..., half_dim:]
    turned = jnp.concatenate(
        [first * cosines - second * sines, second * cosines + first * sines], axis=-1
    )
    return turned.reshape(row_count, -1)


def softmax_rows(scores):
    peak = jnp.max(scores, axis=-1, keepdims=True)
    weights = jnp.exp(scores - peak)
    return weights / jnp.sum(weights, axis=-1, keepdims=True)


def fold_rows(left, piece):
    return jnp.dot(left, piece, preferred_element_type=jnp.float32)


DP_AXES = ("z", "ylo", "x")
MP_AXES = ("yhi", "core")


def gather_dp(flat):
    staged = flat[None]
    for axis in ("x", "ylo", "z"):
        staged = lax.all_gather(staged, axis, axis=0, tiled=True)
    return staged


def per_device(
    tokens,
    attn_gain,
    query_weight,
    key_value_weight,
    query_gain,
    key_gain,
    out_weight,
    ffn_gain,
    gate_up_weight,
    down_weight,
    prompt_lengths,
    page_table,
):
    head_dim = query_gain.shape[0]
    data_groups = 1
    for axis in DP_AXES:
        data_groups *= lax.axis_size(axis)
    part_index = lax.axis_index(MP_AXES)
    own_rows = tokens.shape[0]
    group_tokens = lax.all_gather(tokens, MP_AXES, axis=0, tiled=True)
    row_count = group_tokens.shape[0]
    inputs_wide = group_tokens.astype(jnp.float32)
    normed = rms_rows(inputs_wide, attn_gain).astype(jnp.bfloat16)
    model_width = tokens.shape[1]
    query_cols = query_weight.shape[1]
    keyval_cols = key_value_weight.shape[1]
    kv_rows = lax.all_gather(key_value_weight, MP_AXES, axis=0, tiled=True)
    pieces = [
        query_weight,
        kv_rows,
        out_weight.T,
        gate_up_weight[0],
        gate_up_weight[1],
        down_weight.T,
    ]
    widths = [piece.shape[1] for piece in pieces]
    sizes = [piece.size for piece in pieces]
    packed_weights = jnp.concatenate([piece.astype(jnp.bfloat16).reshape(-1) for piece in pieces])
    gathered = gather_dp(packed_weights)
    offsets = [0]
    for size in sizes:
        offsets.append(offsets[-1] + size)
    def piece_of(k):
        return gathered[:, offsets[k]:offsets[k + 1]].reshape(model_width, widths[k])
    query_full = piece_of(0)
    keyval_full = piece_of(1)
    out_rows_t = piece_of(2)
    gate_full = piece_of(3)
    up_full = piece_of(4)
    down_rows_t = piece_of(5)
    queries = fold_rows(normed, query_full)
    keyvals = fold_rows(normed, keyval_full)
    allowed, cosines, sines = prompt_layout(prompt_lengths[0], row_count, head_dim)
    key_column_width = keyval_cols // 2
    query_heads = rotate_heads(queries, query_gain, cosines, sines).astype(jnp.bfloat16)
    key_head_rows = rotate_heads(keyvals[:, :key_column_width], key_gain, cosines, sines).astype(
        jnp.bfloat16
    )
    value_head_rows = keyvals[:, key_column_width:].astype(jnp.bfloat16)
    cache_rows = jnp.concatenate([key_head_rows, value_head_rows], axis=1)
    pages_here = row_count // PAGE_SLOTS
    cache_pages = cache_rows.reshape(pages_here, PAGE_SLOTS, keyval_cols)
    capacity = pages_here // min(pages_here, data_groups)
    owner = page_table // pages_here
    target = page_table % pages_here
    page_index = jnp.arange(pages_here, dtype=jnp.int32)
    earlier = (owner[None, :] == owner[:, None]) & (page_index[None, :] < page_index[:, None])
    send_slot = owner * capacity + jnp.sum(earlier.astype(jnp.int32), axis=1)
    slot_ids = jnp.arange(data_groups * capacity, dtype=jnp.int32)
    placing = slot_ids[:, None] == send_slot[None, :]
    flat_rows = cache_pages.reshape(pages_here, -1)
    mark_cols = 128
    marks_col = jnp.broadcast_to((target + 1).astype(jnp.bfloat16)[:, None], (pages_here, mark_cols))
    flat_marked = jnp.concatenate([flat_rows, marks_col], axis=1)
    packed = jnp.dot(placing.astype(jnp.bfloat16), flat_marked, preferred_element_type=jnp.float32)
    got_pages = lax.all_to_all(
        packed.astype(jnp.bfloat16).reshape(data_groups, capacity, -1),
        DP_AXES,
        split_axis=0,
        concat_axis=0,
        tiled=True,
    )
    got_flat = got_pages.reshape(data_groups * capacity, -1)
    flat_rows = got_flat[:, : flat_rows.shape[1]]
    got_marks = got_flat[:, flat_rows.shape[1]].astype(jnp.int32)
    choosing = (got_marks[None, :] == page_index[:, None] + 1).astype(jnp.bfloat16)
    kv_pool = (
        jnp.dot(choosing, flat_rows, preferred_element_type=jnp.float32)
        .astype(jnp.bfloat16)
        .reshape(pages_here, PAGE_SLOTS, keyval_cols)
    )
    heads_here = query_cols // head_dim
    shard_portion = QUERY_HEADS // KEYVALUE_HEADS
    kv_heads = key_column_width // head_dim
    global_heads = part_index * heads_here + jnp.arange(heads_here, dtype=jnp.int32)
    source_heads = global_heads // shard_portion
    query_grid = query_heads.reshape(row_count, heads_here, head_dim)
    key_page_grid = jnp.take(
        key_head_rows.reshape(row_count, kv_heads, head_dim), source_heads, axis=1
    )
    value_page_grid = jnp.take(
        value_head_rows.reshape(row_count, kv_heads, head_dim), source_heads, axis=1
    )
    scores = jnp.einsum(
        "qhd,khd->hqk", query_grid, key_page_grid, preferred_element_type=jnp.float32
    ) * head_dim ** (-0.5)
    scores = jnp.where(allowed[None, :, :], scores, -1e30)
    probs = softmax_rows(scores).astype(jnp.bfloat16)
    attended = jnp.einsum(
        "hqk,khd->qhd", probs, value_page_grid, preferred_element_type=jnp.float32
    )
    attended = attended.astype(jnp.bfloat16).reshape(row_count, query_cols)
    attn_part = jnp.einsum("tr,cr->tc", attended, out_rows_t, preferred_element_type=jnp.float32)
    attn_total = lax.psum(attn_part.astype(jnp.bfloat16), MP_AXES).astype(jnp.float32)
    residual_all = inputs_wide + attn_total
    ffn_input = rms_rows(residual_all, ffn_gain).astype(jnp.bfloat16)
    residual_own = lax.dynamic_slice_in_dim(residual_all, part_index * own_rows, own_rows, 0)
    gate = fold_rows(ffn_input, gate_full)
    upward = fold_rows(ffn_input, up_full)
    hidden = (jax.nn.silu(gate) * upward).astype(jnp.bfloat16)
    down_part = jnp.einsum("tf,cf->tc", hidden, down_rows_t, preferred_element_type=jnp.float32)
    layer_out = (
        residual_own
        + lax.psum_scatter(
            down_part.astype(jnp.bfloat16),
            MP_AXES,
            scatter_dimension=0,
            tiled=True,
        ).astype(jnp.float32)
    ).astype(jnp.bfloat16)
    return (layer_out, kv_pool)


def solution(mesh):
    sizes = [mesh.shape["dp"] // (2 * 4), 2, 4, 2, mesh.shape["mp"] // 2]
    fine_mesh = Mesh(mesh.devices.reshape(sizes), DP_AXES + MP_AXES)
    rows = DP_AXES + MP_AXES
    return jax.shard_map(
        per_device,
        mesh=fine_mesh,
        in_specs=(
            P(rows, None),
            P(),
            P(DP_AXES, MP_AXES),
            P(rows, None),
            P(),
            P(),
            P(MP_AXES, DP_AXES),
            P(),
            P(None, DP_AXES, MP_AXES),
            P(MP_AXES, DP_AXES),
            P(DP_AXES, None),
            P(DP_AXES),
        ),
        out_specs=(P(rows, None), P(DP_AXES, None, None)),
        check_vma=False,
    )
```

```python
import jax
import jax.numpy as jnp
from jax import lax
from jax.sharding import Mesh, PartitionSpec as P

QUERY_HEADS = 20
KEYVALUE_HEADS = 5
PAGE_SLOTS = 16


EPSILON = 1e-06


def rms_rows(values, gain):
    scale = lax.rsqrt(jnp.mean(values * values, axis=-1, keepdims=True) + EPSILON)
    return values * scale * gain


def prompt_layout(lengths, row_count, head_dim):
    ends = jnp.cumsum(lengths)
    starts = ends - lengths
    row_index = jnp.arange(row_count, dtype=jnp.int32)
    segment = jnp.sum((row_index[:, None] >= ends[None, :]).astype(jnp.int32), axis=1)
    prompt_ids = jnp.arange(lengths.shape[0], dtype=jnp.int32)
    first_row = jnp.sum(
        jnp.where(segment[:, None] == prompt_ids[None, :], starts[None, :], 0), axis=1
    )
    position = row_index - first_row
    half_dim = head_dim // 2
    frequency = 10000.0 ** (-(jnp.arange(half_dim, dtype=jnp.float32) * (2.0 / head_dim)))
    angle = position.astype(jnp.float32)[:, None] * frequency[None, :]
    allowed = (segment[:, None] == segment[None, :]) & (row_index[None, :] <= row_index[:, None])
    return (allowed, jnp.cos(angle)[:, None, :], jnp.sin(angle)[:, None, :])


def rotate_heads(flat, gain, cosines, sines):
    row_count = flat.shape[0]
    head_dim = gain.shape[0]
    heads = rms_rows(flat.reshape(row_count, -1, head_dim), gain)
    half_dim = head_dim // 2
    first = heads[..., :half_dim]
    second = heads[..., half_dim:]
    turned = jnp.concatenate(
        [first * cosines - second * sines, second * cosines + first * sines], axis=-1
    )
    return turned.reshape(row_count, -1)


def softmax_rows(scores):
    peak = jnp.max(scores, axis=-1, keepdims=True)
    weights = jnp.exp(scores - peak)
    return weights / jnp.sum(weights, axis=-1, keepdims=True)


def fold_rows(left, piece):
    return jnp.dot(left, piece, preferred_element_type=jnp.float32)


DP_AXES = ("z", "ylo", "x")
MP_AXES = ("yhi", "core")


def gather_dp(flat):
    staged = flat[None]
    for axis in ("x", "ylo", "z"):
        staged = lax.all_gather(staged, axis, axis=0, tiled=True)
    return staged


def ring_gather(leaves, axis, count):
    me = lax.axis_index(axis)
    forward_perm = [(i, (i + 1) % count) for i in range(count)]
    backward_perm = [(i, (i - 1) % count) for i in range(count)]
    chunks = {0: leaves}
    ahead = leaves
    behind = leaves
    for step in range(1, count // 2 + 1):
        if count == 2:
            chunks[1] = lax.ppermute(leaves, axis, forward_perm)
        elif step < count - step:
            ahead = lax.ppermute(ahead, axis, forward_perm)
            behind = lax.ppermute(behind, axis, backward_perm)
            chunks[count - step] = ahead
            chunks[step] = behind
        else:
            halves = [leaf.shape[-1] // 2 for leaf in leaves]
            first = lax.ppermute(
                [leaf[..., :h] for leaf, h in zip(ahead, halves)], axis, forward_perm
            )
            second = lax.ppermute(
                [leaf[..., h:] for leaf, h in zip(behind, halves)], axis, backward_perm
            )
            chunks[step] = [jnp.concatenate([a, b], axis=-1) for a, b in zip(first, second)]
    out = []
    for k, leaf in enumerate(leaves):
        lead = leaf.shape[:-1]
        full = jnp.zeros(lead + (count, leaf.shape[-1]), leaf.dtype)
        for r, got in chunks.items():
            at = (0,) * len(lead) + ((me + r) % count, 0)
            full = lax.dynamic_update_slice(full, got[k][..., None, :], at)
        out.append(full)
    return out


def per_device(
    tokens,
    attn_gain,
    query_weight,
    key_value_weight,
    query_gain,
    key_gain,
    out_weight,
    ffn_gain,
    gate_up_weight,
    down_weight,
    prompt_lengths,
    page_table,
):
    head_dim = query_gain.shape[0]
    data_groups = 1
    for axis in DP_AXES:
        data_groups *= lax.axis_size(axis)
    part_index = lax.axis_index(MP_AXES)
    own_rows = tokens.shape[0]
    group_tokens = lax.all_gather(tokens, MP_AXES, axis=0, tiled=True)
    row_count = group_tokens.shape[0]
    inputs_wide = group_tokens.astype(jnp.float32)
    normed = rms_rows(inputs_wide, attn_gain).astype(jnp.bfloat16)
    model_width = tokens.shape[1]
    query_cols = query_weight.shape[1]
    keyval_cols = key_value_weight.shape[1]
    kv_rows = lax.all_gather(key_value_weight, MP_AXES, axis=0, tiled=True)
    ring_leaves = [
        query_weight.astype(jnp.bfloat16),
        kv_rows.astype(jnp.bfloat16),
        out_weight.T.astype(jnp.bfloat16),
        down_weight.T.astype(jnp.bfloat16),
    ]
    widths = [leaf.shape[1] for leaf in ring_leaves]
    ring_sizes = [leaf.size for leaf in ring_leaves]
    ring_flat = [jnp.concatenate([leaf.reshape(-1) for leaf in ring_leaves])]
    ring_flat = ring_gather(ring_flat, "z", lax.axis_size("z"))
    ring_flat = ring_gather(ring_flat, "ylo", lax.axis_size("ylo"))
    ring_flat = ring_gather(ring_flat, "x", lax.axis_size("x"))
    ring_all = ring_flat[0].reshape(data_groups, -1)
    ring_offsets = [0]
    for size in ring_sizes:
        ring_offsets.append(ring_offsets[-1] + size)
    query_full, keyval_full, out_rows_t, down_rows_t = [
        ring_all[:, ring_offsets[k]:ring_offsets[k + 1]].reshape(model_width, widths[k])
        for k in range(len(widths))
    ]
    ffn_pieces = [gate_up_weight[0], gate_up_weight[1]]
    ffn_size = ffn_pieces[0].size
    packed_weights = jnp.concatenate([piece.astype(jnp.bfloat16).reshape(-1) for piece in ffn_pieces])
    gathered = gather_dp(packed_weights)
    ffn_width = gate_up_weight.shape[2]
    gate_full = gathered[:, :ffn_size].reshape(model_width, ffn_width)
    up_full = gathered[:, ffn_size:].reshape(model_width, ffn_width)
    queries = fold_rows(normed, query_full)
    keyvals = fold_rows(normed, keyval_full)
    allowed, cosines, sines = prompt_layout(prompt_lengths[0], row_count, head_dim)
    key_column_width = keyval_cols // 2
    query_heads = rotate_heads(queries, query_gain, cosines, sines).astype(jnp.bfloat16)
    key_head_rows = rotate_heads(keyvals[:, :key_column_width], key_gain, cosines, sines).astype(
        jnp.bfloat16
    )
    value_head_rows = keyvals[:, key_column_width:].astype(jnp.bfloat16)
    cache_rows = jnp.concatenate([key_head_rows, value_head_rows], axis=1)
    pages_here = row_count // PAGE_SLOTS
    cache_pages = cache_rows.reshape(pages_here, PAGE_SLOTS, keyval_cols)
    capacity = pages_here // min(pages_here, data_groups)
    owner = page_table // pages_here
    target = page_table % pages_here
    page_index = jnp.arange(pages_here, dtype=jnp.int32)
    earlier = (owner[None, :] == owner[:, None]) & (page_index[None, :] < page_index[:, None])
    send_slot = owner * capacity + jnp.sum(earlier.astype(jnp.int32), axis=1)
    slot_ids = jnp.arange(data_groups * capacity, dtype=jnp.int32)
    placing = slot_ids[:, None] == send_slot[None, :]
    flat_rows = cache_pages.reshape(pages_here, -1)
    mark_cols = 128
    marks_col = jnp.broadcast_to((target + 1).astype(jnp.bfloat16)[:, None], (pages_here, mark_cols))
    flat_marked = jnp.concatenate([flat_rows, marks_col], axis=1)
    packed = jnp.dot(placing.astype(jnp.bfloat16), flat_marked, preferred_element_type=jnp.float32)
    got_pages = lax.all_to_all(
        packed.astype(jnp.bfloat16).reshape(data_groups, capacity, -1),
        DP_AXES,
        split_axis=0,
        concat_axis=0,
        tiled=True,
    )
    got_flat = got_pages.reshape(data_groups * capacity, -1)
    flat_rows = got_flat[:, : flat_rows.shape[1]]
    got_marks = got_flat[:, flat_rows.shape[1]].astype(jnp.int32)
    choosing = (got_marks[None, :] == page_index[:, None] + 1).astype(jnp.bfloat16)
    kv_pool = (
        jnp.dot(choosing, flat_rows, preferred_element_type=jnp.float32)
        .astype(jnp.bfloat16)
        .reshape(pages_here, PAGE_SLOTS, keyval_cols)
    )
    heads_here = query_cols // head_dim
    shard_portion = QUERY_HEADS // KEYVALUE_HEADS
    kv_heads = key_column_width // head_dim
    global_heads = part_index * heads_here + jnp.arange(heads_here, dtype=jnp.int32)
    source_heads = global_heads // shard_portion
    query_grid = query_heads.reshape(row_count, heads_here, head_dim)
    key_page_grid = jnp.take(
        key_head_rows.reshape(row_count, kv_heads, head_dim), source_heads, axis=1
    )
    value_page_grid = jnp.take(
        value_head_rows.reshape(row_count, kv_heads, head_dim), source_heads, axis=1
    )
    scores = jnp.einsum(
        "qhd,khd->hqk", query_grid, key_page_grid, preferred_element_type=jnp.float32
    ) * head_dim ** (-0.5)
    scores = jnp.where(allowed[None, :, :], scores, -1e30)
    probs = softmax_rows(scores).astype(jnp.bfloat16)
    attended = jnp.einsum(
        "hqk,khd->qhd", probs, value_page_grid, preferred_element_type=jnp.float32
    )
    attended = attended.astype(jnp.bfloat16).reshape(row_count, query_cols)
    attn_part = jnp.einsum("tr,cr->tc", attended, out_rows_t, preferred_element_type=jnp.float32)
    attn_total = lax.psum(attn_part.astype(jnp.bfloat16), MP_AXES).astype(jnp.float32)
    residual_all = inputs_wide + attn_total
    ffn_input = rms_rows(residual_all, ffn_gain).astype(jnp.bfloat16)
    residual_own = lax.dynamic_slice_in_dim(residual_all, part_index * own_rows, own_rows, 0)
    gate = fold_rows(ffn_input, gate_full)
    upward = fold_rows(ffn_input, up_full)
    hidden = (jax.nn.silu(gate) * upward).astype(jnp.bfloat16)
    down_part = jnp.einsum("tf,cf->tc", hidden, down_rows_t, preferred_element_type=jnp.float32)
    layer_out = (
        residual_own
        + lax.psum_scatter(
            down_part.astype(jnp.bfloat16),
            MP_AXES,
            scatter_dimension=0,
            tiled=True,
        ).astype(jnp.float32)
    ).astype(jnp.bfloat16)
    return (layer_out, kv_pool)


def solution(mesh):
    sizes = [mesh.shape["dp"] // (2 * 4), 2, 4, 2, mesh.shape["mp"] // 2]
    fine_mesh = Mesh(mesh.devices.reshape(sizes), DP_AXES + MP_AXES)
    rows = DP_AXES + MP_AXES
    return jax.shard_map(
        per_device,
        mesh=fine_mesh,
        in_specs=(
            P(rows, None),
            P(),
            P(DP_AXES, MP_AXES),
            P(rows, None),
            P(),
            P(),
            P(MP_AXES, DP_AXES),
            P(),
            P(None, DP_AXES, MP_AXES),
            P(MP_AXES, DP_AXES),
            P(DP_AXES, None),
            P(DP_AXES),
        ),
        out_specs=(P(rows, None), P(DP_AXES, None, None)),
        check_vma=False,
    )
```

```python
import jax
import jax.numpy as jnp
from jax import lax
from jax.sharding import Mesh, PartitionSpec as P

QUERY_HEADS = 20
KEYVALUE_HEADS = 5
PAGE_SLOTS = 16


EPSILON = 1e-06


def rms_rows(values, gain):
    scale = lax.rsqrt(jnp.mean(values * values, axis=-1, keepdims=True) + EPSILON)
    return values * scale * gain


def prompt_layout(lengths, row_count, head_dim):
    ends = jnp.cumsum(lengths)
    starts = ends - lengths
    row_index = jnp.arange(row_count, dtype=jnp.int32)
    segment = jnp.sum((row_index[:, None] >= ends[None, :]).astype(jnp.int32), axis=1)
    prompt_ids = jnp.arange(lengths.shape[0], dtype=jnp.int32)
    first_row = jnp.sum(
        jnp.where(segment[:, None] == prompt_ids[None, :], starts[None, :], 0), axis=1
    )
    position = row_index - first_row
    half_dim = head_dim // 2
    frequency = 10000.0 ** (-(jnp.arange(half_dim, dtype=jnp.float32) * (2.0 / head_dim)))
    angle = position.astype(jnp.float32)[:, None] * frequency[None, :]
    allowed = (segment[:, None] == segment[None, :]) & (row_index[None, :] <= row_index[:, None])
    return (allowed, jnp.cos(angle)[:, None, :], jnp.sin(angle)[:, None, :])


def rotate_heads(flat, gain, cosines, sines):
    row_count = flat.shape[0]
    head_dim = gain.shape[0]
    heads = rms_rows(flat.reshape(row_count, -1, head_dim), gain)
    half_dim = head_dim // 2
    first = heads[..., :half_dim]
    second = heads[..., half_dim:]
    turned = jnp.concatenate(
        [first * cosines - second * sines, second * cosines + first * sines], axis=-1
    )
    return turned.reshape(row_count, -1)


def softmax_rows(scores):
    peak = jnp.max(scores, axis=-1, keepdims=True)
    weights = jnp.exp(scores - peak)
    return weights / jnp.sum(weights, axis=-1, keepdims=True)


def fold_rows(left, piece):
    return jnp.dot(left, piece, preferred_element_type=jnp.float32)


DP_AXES = ("z", "ylo", "x")
MP_AXES = ("yhi", "core")


def gather_dp(flat):
    staged = flat[None]
    for axis in ("x", "ylo", "z"):
        staged = lax.all_gather(staged, axis, axis=0, tiled=True)
    return staged


def ring_gather(block, axis, count, at):
    forward_perm = [(i, (i + 1) % count) for i in range(count)]
    backward_perm = [(i, (i - 1) % count) for i in range(count)]
    chunks = {0: block}
    ahead = block
    behind = block
    for step in range(1, count // 2 + 1):
        if count == 2:
            chunks[1] = lax.ppermute(block, axis, forward_perm)
        elif step < count - step:
            ahead = lax.ppermute(ahead, axis, forward_perm)
            behind = lax.ppermute(behind, axis, backward_perm)
            chunks[count - step] = ahead
            chunks[step] = behind
        else:
            half = block.shape[-1] // 2
            first = lax.ppermute(ahead[..., :half], axis, forward_perm)
            second = lax.ppermute(behind[..., half:], axis, backward_perm)
            chunks[step] = jnp.concatenate([first, second], axis=-1)
    return jnp.stack([chunks[r] for r in range(count)], axis=at)


def to_relative(values, inverse=False):
    lead = values.shape[:-1]
    sizes = [lax.axis_size(axis) for axis in DP_AXES]
    grid = values.reshape(lead + tuple(sizes) + (-1,))
    for k, axis in enumerate(DP_AXES):
        shift = lax.axis_index(axis)
        grid = jnp.roll(grid, shift if inverse else -shift, axis=len(lead) + k)
    return grid.reshape(values.shape)


def per_device(
    tokens,
    attn_gain,
    query_weight,
    key_value_weight,
    query_gain,
    key_gain,
    out_weight,
    ffn_gain,
    gate_up_weight,
    down_weight,
    prompt_lengths,
    page_table,
):
    head_dim = query_gain.shape[0]
    data_groups = 1
    for axis in DP_AXES:
        data_groups *= lax.axis_size(axis)
    part_index = lax.axis_index(MP_AXES)
    own_rows = tokens.shape[0]
    group_tokens = lax.all_gather(tokens, MP_AXES, axis=0, tiled=True)
    row_count = group_tokens.shape[0]
    inputs_wide = group_tokens.astype(jnp.float32)
    normed = rms_rows(inputs_wide, attn_gain).astype(jnp.bfloat16)
    model_width = tokens.shape[1]
    query_cols = query_weight.shape[1]
    keyval_cols = key_value_weight.shape[1]
    kv_rows = lax.all_gather(key_value_weight, MP_AXES, axis=0, tiled=True)
    pieces = [
        query_weight,
        kv_rows,
        out_weight.T,
        gate_up_weight[0],
    ]
    widths = [piece.shape[1] for piece in pieces]
    sizes = [piece.size for piece in pieces]
    packed_weights = jnp.concatenate([piece.astype(jnp.bfloat16).reshape(-1) for piece in pieces])
    gathered = gather_dp(packed_weights)
    offsets = [0]
    for size in sizes:
        offsets.append(offsets[-1] + size)
    def piece_of(k):
        return gathered[:, offsets[k]:offsets[k + 1]].reshape(model_width, widths[k])
    query_full = piece_of(0)
    keyval_full = piece_of(1)
    out_rows_t = piece_of(2)
    gate_full = piece_of(3)
    ring_pieces = [gate_up_weight[1], down_weight.T]
    ring_size = ring_pieces[0].size
    ring_block = jnp.concatenate([piece.astype(jnp.bfloat16).reshape(-1) for piece in ring_pieces])
    for k, axis in enumerate(DP_AXES):
        ring_block = ring_gather(ring_block, axis, lax.axis_size(axis), k)
    ring_all = ring_block.reshape(data_groups, -1)
    ffn_width = gate_up_weight.shape[2]
    up_relative = ring_all[:, :ring_size].reshape(model_width, ffn_width)
    down_relative_t = ring_all[:, ring_size:].reshape(model_width, ffn_width)
    queries = fold_rows(normed, query_full)
    keyvals = fold_rows(normed, keyval_full)
    allowed, cosines, sines = prompt_layout(prompt_lengths[0], row_count, head_dim)
    key_column_width = keyval_cols // 2
    query_heads = rotate_heads(queries, query_gain, cosines, sines).astype(jnp.bfloat16)
    key_head_rows = rotate_heads(keyvals[:, :key_column_width], key_gain, cosines, sines).astype(
        jnp.bfloat16
    )
    value_head_rows = keyvals[:, key_column_width:].astype(jnp.bfloat16)
    cache_rows = jnp.concatenate([key_head_rows, value_head_rows], axis=1)
    pages_here = row_count // PAGE_SLOTS
    cache_pages = cache_rows.reshape(pages_here, PAGE_SLOTS, keyval_cols)
    capacity = pages_here // min(pages_here, data_groups)
    owner = page_table // pages_here
    target = page_table % pages_here
    page_index = jnp.arange(pages_here, dtype=jnp.int32)
    earlier = (owner[None, :] == owner[:, None]) & (page_index[None, :] < page_index[:, None])
    send_slot = owner * capacity + jnp.sum(earlier.astype(jnp.int32), axis=1)
    slot_ids = jnp.arange(data_groups * capacity, dtype=jnp.int32)
    placing = slot_ids[:, None] == send_slot[None, :]
    flat_rows = cache_pages.reshape(pages_here, -1)
    mark_cols = 128
    marks_col = jnp.broadcast_to((target + 1).astype(jnp.bfloat16)[:, None], (pages_here, mark_cols))
    flat_marked = jnp.concatenate([flat_rows, marks_col], axis=1)
    packed = jnp.dot(placing.astype(jnp.bfloat16), flat_marked, preferred_element_type=jnp.float32)
    got_pages = lax.all_to_all(
        packed.astype(jnp.bfloat16).reshape(data_groups, capacity, -1),
        DP_AXES,
        split_axis=0,
        concat_axis=0,
        tiled=True,
    )
    got_flat = got_pages.reshape(data_groups * capacity, -1)
    flat_rows = got_flat[:, : flat_rows.shape[1]]
    got_marks = got_flat[:, flat_rows.shape[1]].astype(jnp.int32)
    choosing = (got_marks[None, :] == page_index[:, None] + 1).astype(jnp.bfloat16)
    kv_pool = (
        jnp.dot(choosing, flat_rows, preferred_element_type=jnp.float32)
        .astype(jnp.bfloat16)
        .reshape(pages_here, PAGE_SLOTS, keyval_cols)
    )
    heads_here = query_cols // head_dim
    shard_portion = QUERY_HEADS // KEYVALUE_HEADS
    kv_heads = key_column_width // head_dim
    global_heads = part_index * heads_here + jnp.arange(heads_here, dtype=jnp.int32)
    source_heads = global_heads // shard_portion
    query_grid = query_heads.reshape(row_count, heads_here, head_dim)
    key_page_grid = jnp.take(
        key_head_rows.reshape(row_count, kv_heads, head_dim), source_heads, axis=1
    )
    value_page_grid = jnp.take(
        value_head_rows.reshape(row_count, kv_heads, head_dim), source_heads, axis=1
    )
    scores = jnp.einsum(
        "qhd,khd->hqk", query_grid, key_page_grid, preferred_element_type=jnp.float32
    ) * head_dim ** (-0.5)
    scores = jnp.where(allowed[None, :, :], scores, -1e30)
    probs = softmax_rows(scores).astype(jnp.bfloat16)
    attended = jnp.einsum(
        "hqk,khd->qhd", probs, value_page_grid, preferred_element_type=jnp.float32
    )
    attended = attended.astype(jnp.bfloat16).reshape(row_count, query_cols)
    attn_part = jnp.einsum("tr,cr->tc", attended, out_rows_t, preferred_element_type=jnp.float32)
    attn_total = lax.psum(attn_part.astype(jnp.bfloat16), MP_AXES).astype(jnp.float32)
    residual_all = inputs_wide + attn_total
    ffn_input = rms_rows(residual_all, ffn_gain).astype(jnp.bfloat16)
    residual_own = lax.dynamic_slice_in_dim(residual_all, part_index * own_rows, own_rows, 0)
    gate = fold_rows(ffn_input, gate_full)
    upward = fold_rows(to_relative(ffn_input), up_relative)
    hidden = (jax.nn.silu(gate) * upward).astype(jnp.bfloat16)
    down_part = to_relative(
        jnp.einsum("tf,cf->tc", hidden, down_relative_t, preferred_element_type=jnp.float32),
        inverse=True,
    )
    layer_out = (
        residual_own
        + lax.psum_scatter(
            down_part.astype(jnp.bfloat16),
            MP_AXES,
            scatter_dimension=0,
            tiled=True,
        ).astype(jnp.float32)
    ).astype(jnp.bfloat16)
    return (layer_out, kv_pool)


def solution(mesh):
    sizes = [mesh.shape["dp"] // (2 * 4), 2, 4, 2, mesh.shape["mp"] // 2]
    fine_mesh = Mesh(mesh.devices.reshape(sizes), DP_AXES + MP_AXES)
    rows = DP_AXES + MP_AXES
    return jax.shard_map(
        per_device,
        mesh=fine_mesh,
        in_specs=(
            P(rows, None),
            P(),
            P(DP_AXES, MP_AXES),
            P(rows, None),
            P(),
            P(),
            P(MP_AXES, DP_AXES),
            P(),
            P(None, DP_AXES, MP_AXES),
            P(MP_AXES, DP_AXES),
            P(DP_AXES, None),
            P(DP_AXES),
        ),
        out_specs=(P(rows, None), P(DP_AXES, None, None)),
        check_vma=False,
    )
```

```python
import jax
import jax.numpy as jnp
from jax import lax
from jax.sharding import Mesh, PartitionSpec as P

QUERY_HEADS = 20
KEYVALUE_HEADS = 5
PAGE_SLOTS = 16


EPSILON = 1e-06


def rms_rows(values, gain):
    scale = lax.rsqrt(jnp.mean(values * values, axis=-1, keepdims=True) + EPSILON)
    return values * scale * gain


def prompt_layout(lengths, row_count, head_dim):
    ends = jnp.cumsum(lengths)
    starts = ends - lengths
    row_index = jnp.arange(row_count, dtype=jnp.int32)
    segment = jnp.sum((row_index[:, None] >= ends[None, :]).astype(jnp.int32), axis=1)
    prompt_ids = jnp.arange(lengths.shape[0], dtype=jnp.int32)
    first_row = jnp.sum(
        jnp.where(segment[:, None] == prompt_ids[None, :], starts[None, :], 0), axis=1
    )
    position = row_index - first_row
    half_dim = head_dim // 2
    frequency = 10000.0 ** (-(jnp.arange(half_dim, dtype=jnp.float32) * (2.0 / head_dim)))
    angle = position.astype(jnp.float32)[:, None] * frequency[None, :]
    allowed = (segment[:, None] == segment[None, :]) & (row_index[None, :] <= row_index[:, None])
    return (allowed, jnp.cos(angle)[:, None, :], jnp.sin(angle)[:, None, :])


def rotate_heads(flat, gain, cosines, sines):
    row_count = flat.shape[0]
    head_dim = gain.shape[0]
    heads = rms_rows(flat.reshape(row_count, -1, head_dim), gain)
    half_dim = head_dim // 2
    first = heads[..., :half_dim]
    second = heads[..., half_dim:]
    turned = jnp.concatenate(
        [first * cosines - second * sines, second * cosines + first * sines], axis=-1
    )
    return turned.reshape(row_count, -1)


def softmax_rows(scores):
    peak = jnp.max(scores, axis=-1, keepdims=True)
    weights = jnp.exp(scores - peak)
    return weights / jnp.sum(weights, axis=-1, keepdims=True)


def fold_rows(left, piece):
    return jnp.dot(left, piece, preferred_element_type=jnp.float32)


DP_AXES = ("z", "ylo", "x")
MP_AXES = ("yhi", "core")


def gather_dp(flat):
    staged = ring_gather(flat, "x", lax.axis_size("x"), 0)
    for axis in ("ylo", "z"):
        staged = lax.all_gather(staged, axis, axis=0, tiled=True)
    return staged


def ring_gather(block, axis, count, at):
    forward_perm = [(i, (i + 1) % count) for i in range(count)]
    backward_perm = [(i, (i - 1) % count) for i in range(count)]
    chunks = {0: block}
    ahead = block
    behind = block
    for step in range(1, count // 2 + 1):
        if count == 2:
            chunks[1] = lax.ppermute(block, axis, forward_perm)
        elif step < count - step:
            ahead = lax.ppermute(ahead, axis, forward_perm)
            behind = lax.ppermute(behind, axis, backward_perm)
            chunks[count - step] = ahead
            chunks[step] = behind
        else:
            half = block.shape[-1] // 2
            first = lax.ppermute(ahead[..., :half], axis, forward_perm)
            second = lax.ppermute(behind[..., half:], axis, backward_perm)
            chunks[step] = jnp.concatenate([first, second], axis=-1)
    return jnp.stack([chunks[r] for r in range(count)], axis=at)


def to_relative(values, inverse=False, axes=DP_AXES):
    lead = values.shape[:-1]
    sizes = [lax.axis_size(axis) for axis in DP_AXES]
    grid = values.reshape(lead + tuple(sizes) + (-1,))
    for k, axis in enumerate(DP_AXES):
        if axis not in axes:
            continue
        shift = lax.axis_index(axis)
        grid = jnp.roll(grid, shift if inverse else -shift, axis=len(lead) + k)
    return grid.reshape(values.shape)


def per_device(
    tokens,
    attn_gain,
    query_weight,
    key_value_weight,
    query_gain,
    key_gain,
    out_weight,
    ffn_gain,
    gate_up_weight,
    down_weight,
    prompt_lengths,
    page_table,
):
    head_dim = query_gain.shape[0]
    data_groups = 1
    for axis in DP_AXES:
        data_groups *= lax.axis_size(axis)
    part_index = lax.axis_index(MP_AXES)
    own_rows = tokens.shape[0]
    group_tokens = lax.all_gather(tokens, MP_AXES, axis=0, tiled=True)
    row_count = group_tokens.shape[0]
    inputs_wide = group_tokens.astype(jnp.float32)
    normed = rms_rows(inputs_wide, attn_gain).astype(jnp.bfloat16)
    model_width = tokens.shape[1]
    query_cols = query_weight.shape[1]
    keyval_cols = key_value_weight.shape[1]
    kv_rows = lax.all_gather(key_value_weight, MP_AXES, axis=0, tiled=True)
    pieces = [
        query_weight,
        kv_rows,
        out_weight.T,
        gate_up_weight[0],
    ]
    widths = [piece.shape[1] for piece in pieces]
    sizes = [piece.size for piece in pieces]
    packed_weights = jnp.concatenate([piece.astype(jnp.bfloat16).reshape(-1) for piece in pieces])
    gathered = gather_dp(packed_weights)
    offsets = [0]
    for size in sizes:
        offsets.append(offsets[-1] + size)
    def piece_of(k):
        return gathered[:, offsets[k]:offsets[k + 1]].reshape(model_width, widths[k])
    query_full = piece_of(0)
    keyval_full = piece_of(1)
    out_rows_t = piece_of(2)
    gate_full = piece_of(3)
    ring_pieces = [gate_up_weight[1], down_weight.T]
    ring_size = ring_pieces[0].size
    ring_block = jnp.concatenate([piece.astype(jnp.bfloat16).reshape(-1) for piece in ring_pieces])
    for k, axis in enumerate(DP_AXES):
        ring_block = ring_gather(ring_block, axis, lax.axis_size(axis), k)
    ring_all = ring_block.reshape(data_groups, -1)
    ffn_width = gate_up_weight.shape[2]
    up_relative = ring_all[:, :ring_size].reshape(model_width, ffn_width)
    down_relative_t = ring_all[:, ring_size:].reshape(model_width, ffn_width)
    normed_x = to_relative(normed, axes=("x",))
    queries = fold_rows(normed_x, query_full)
    keyvals = fold_rows(normed_x, keyval_full)
    allowed, cosines, sines = prompt_layout(prompt_lengths[0], row_count, head_dim)
    key_column_width = keyval_cols // 2
    query_heads = rotate_heads(queries, query_gain, cosines, sines).astype(jnp.bfloat16)
    key_head_rows = rotate_heads(keyvals[:, :key_column_width], key_gain, cosines, sines).astype(
        jnp.bfloat16
    )
    value_head_rows = keyvals[:, key_column_width:].astype(jnp.bfloat16)
    cache_rows = jnp.concatenate([key_head_rows, value_head_rows], axis=1)
    pages_here = row_count // PAGE_SLOTS
    cache_pages = cache_rows.reshape(pages_here, PAGE_SLOTS, keyval_cols)
    capacity = pages_here // min(pages_here, data_groups)
    owner = page_table // pages_here
    target = page_table % pages_here
    page_index = jnp.arange(pages_here, dtype=jnp.int32)
    earlier = (owner[None, :] == owner[:, None]) & (page_index[None, :] < page_index[:, None])
    send_slot = owner * capacity + jnp.sum(earlier.astype(jnp.int32), axis=1)
    slot_ids = jnp.arange(data_groups * capacity, dtype=jnp.int32)
    placing = slot_ids[:, None] == send_slot[None, :]
    flat_rows = cache_pages.reshape(pages_here, -1)
    mark_cols = 128
    marks_col = jnp.broadcast_to((target + 1).astype(jnp.bfloat16)[:, None], (pages_here, mark_cols))
    flat_marked = jnp.concatenate([flat_rows, marks_col], axis=1)
    packed = jnp.dot(placing.astype(jnp.bfloat16), flat_marked, preferred_element_type=jnp.float32)
    got_pages = lax.all_to_all(
        packed.astype(jnp.bfloat16).reshape(data_groups, capacity, -1),
        DP_AXES,
        split_axis=0,
        concat_axis=0,
        tiled=True,
    )
    got_flat = got_pages.reshape(data_groups * capacity, -1)
    flat_rows = got_flat[:, : flat_rows.shape[1]]
    got_marks = got_flat[:, flat_rows.shape[1]].astype(jnp.int32)
    choosing = (got_marks[None, :] == page_index[:, None] + 1).astype(jnp.bfloat16)
    kv_pool = (
        jnp.dot(choosing, flat_rows, preferred_element_type=jnp.float32)
        .astype(jnp.bfloat16)
        .reshape(pages_here, PAGE_SLOTS, keyval_cols)
    )
    heads_here = query_cols // head_dim
    shard_portion = QUERY_HEADS // KEYVALUE_HEADS
    kv_heads = key_column_width // head_dim
    global_heads = part_index * heads_here + jnp.arange(heads_here, dtype=jnp.int32)
    source_heads = global_heads // shard_portion
    query_grid = query_heads.reshape(row_count, heads_here, head_dim)
    key_page_grid = jnp.take(
        key_head_rows.reshape(row_count, kv_heads, head_dim), source_heads, axis=1
    )
    value_page_grid = jnp.take(
        value_head_rows.reshape(row_count, kv_heads, head_dim), source_heads, axis=1
    )
    scores = jnp.einsum(
        "qhd,khd->hqk", query_grid, key_page_grid, preferred_element_type=jnp.float32
    ) * head_dim ** (-0.5)
    scores = jnp.where(allowed[None, :, :], scores, -1e30)
    probs = softmax_rows(scores).astype(jnp.bfloat16)
    attended = jnp.einsum(
        "hqk,khd->qhd", probs, value_page_grid, preferred_element_type=jnp.float32
    )
    attended = attended.astype(jnp.bfloat16).reshape(row_count, query_cols)
    attn_part = to_relative(
        jnp.einsum("tr,cr->tc", attended, out_rows_t, preferred_element_type=jnp.float32),
        inverse=True,
        axes=("x",),
    )
    attn_total = lax.psum(attn_part.astype(jnp.bfloat16), MP_AXES).astype(jnp.float32)
    residual_all = inputs_wide + attn_total
    ffn_input = rms_rows(residual_all, ffn_gain).astype(jnp.bfloat16)
    residual_own = lax.dynamic_slice_in_dim(residual_all, part_index * own_rows, own_rows, 0)
    gate = fold_rows(to_relative(ffn_input, axes=("x",)), gate_full)
    upward = fold_rows(to_relative(ffn_input), up_relative)
    hidden = (jax.nn.silu(gate) * upward).astype(jnp.bfloat16)
    down_part = to_relative(
        jnp.einsum("tf,cf->tc", hidden, down_relative_t, preferred_element_type=jnp.float32),
        inverse=True,
    )
    layer_out = (
        residual_own
        + lax.psum_scatter(
            down_part.astype(jnp.bfloat16),
            MP_AXES,
            scatter_dimension=0,
            tiled=True,
        ).astype(jnp.float32)
    ).astype(jnp.bfloat16)
    return (layer_out, kv_pool)


def solution(mesh):
    sizes = [mesh.shape["dp"] // (2 * 4), 2, 4, 2, mesh.shape["mp"] // 2]
    fine_mesh = Mesh(mesh.devices.reshape(sizes), DP_AXES + MP_AXES)
    rows = DP_AXES + MP_AXES
    return jax.shard_map(
        per_device,
        mesh=fine_mesh,
        in_specs=(
            P(rows, None),
            P(),
            P(DP_AXES, MP_AXES),
            P(rows, None),
            P(),
            P(),
            P(MP_AXES, DP_AXES),
            P(),
            P(None, DP_AXES, MP_AXES),
            P(MP_AXES, DP_AXES),
            P(DP_AXES, None),
            P(DP_AXES),
        ),
        out_specs=(P(rows, None), P(DP_AXES, None, None)),
        check_vma=False,
    )
```

```python
import jax
import jax.numpy as jnp
from jax import lax
from jax.sharding import Mesh, PartitionSpec as P

QUERY_HEADS = 20
KEYVALUE_HEADS = 5
PAGE_SLOTS = 16


EPSILON = 1e-06


def rms_rows(values, gain):
    scale = lax.rsqrt(jnp.mean(values * values, axis=-1, keepdims=True) + EPSILON)
    return values * scale * gain


def prompt_layout(lengths, row_count, head_dim):
    ends = jnp.cumsum(lengths)
    starts = ends - lengths
    row_index = jnp.arange(row_count, dtype=jnp.int32)
    segment = jnp.sum((row_index[:, None] >= ends[None, :]).astype(jnp.int32), axis=1)
    prompt_ids = jnp.arange(lengths.shape[0], dtype=jnp.int32)
    first_row = jnp.sum(
        jnp.where(segment[:, None] == prompt_ids[None, :], starts[None, :], 0), axis=1
    )
    position = row_index - first_row
    half_dim = head_dim // 2
    frequency = 10000.0 ** (-(jnp.arange(half_dim, dtype=jnp.float32) * (2.0 / head_dim)))
    angle = position.astype(jnp.float32)[:, None] * frequency[None, :]
    allowed = (segment[:, None] == segment[None, :]) & (row_index[None, :] <= row_index[:, None])
    return (allowed, jnp.cos(angle)[:, None, :], jnp.sin(angle)[:, None, :])


def rotate_heads(flat, gain, cosines, sines):
    row_count = flat.shape[0]
    head_dim = gain.shape[0]
    heads = rms_rows(flat.reshape(row_count, -1, head_dim), gain)
    half_dim = head_dim // 2
    first = heads[..., :half_dim]
    second = heads[..., half_dim:]
    turned = jnp.concatenate(
        [first * cosines - second * sines, second * cosines + first * sines], axis=-1
    )
    return turned.reshape(row_count, -1)


def softmax_rows(scores):
    peak = jnp.max(scores, axis=-1, keepdims=True)
    weights = jnp.exp(scores - peak)
    return weights / jnp.sum(weights, axis=-1, keepdims=True)


def fold_rows(left, piece):
    return jnp.dot(left, piece, preferred_element_type=jnp.float32)


DP_AXES = ("z", "ylo", "x")
MP_AXES = ("yhi", "core")


def gather_dp(flat):
    staged = ring_gather(flat, "x", lax.axis_size("x"), 0)
    for axis in ("ylo", "z"):
        staged = lax.all_gather(staged, axis, axis=0, tiled=True)
    return staged


def ring_gather(block, axis, count, at):
    forward_perm = [(i, (i + 1) % count) for i in range(count)]
    backward_perm = [(i, (i - 1) % count) for i in range(count)]
    chunks = {0: block}
    ahead = block
    behind = block
    for step in range(1, count // 2 + 1):
        if count == 2:
            chunks[1] = lax.ppermute(block, axis, forward_perm)
        elif step < count - step:
            ahead = lax.ppermute(ahead, axis, forward_perm)
            behind = lax.ppermute(behind, axis, backward_perm)
            chunks[count - step] = ahead
            chunks[step] = behind
        else:
            half = block.shape[-1] // 2
            first = lax.ppermute(ahead[..., :half], axis, forward_perm)
            second = lax.ppermute(behind[..., half:], axis, backward_perm)
            chunks[step] = jnp.concatenate([first, second], axis=-1)
    return jnp.stack([chunks[r] for r in range(count)], axis=at)


def to_relative(values, inverse=False, axes=DP_AXES):
    lead = values.shape[:-1]
    sizes = [lax.axis_size(axis) for axis in DP_AXES]
    grid = values.reshape(lead + tuple(sizes) + (-1,))
    for k, axis in enumerate(DP_AXES):
        if axis not in axes:
            continue
        shift = lax.axis_index(axis)
        grid = jnp.roll(grid, shift if inverse else -shift, axis=len(lead) + k)
    return grid.reshape(values.shape)


def per_device(
    tokens,
    attn_gain,
    query_weight,
    key_value_weight,
    query_gain,
    key_gain,
    out_weight,
    ffn_gain,
    gate_up_weight,
    down_weight,
    prompt_lengths,
    page_table,
):
    head_dim = query_gain.shape[0]
    data_groups = 1
    for axis in DP_AXES:
        data_groups *= lax.axis_size(axis)
    part_index = lax.axis_index(MP_AXES)
    own_rows = tokens.shape[0]
    group_tokens = lax.all_gather(tokens, MP_AXES, axis=0, tiled=True)
    row_count = group_tokens.shape[0]
    inputs_wide = group_tokens.astype(jnp.float32)
    normed = rms_rows(inputs_wide, attn_gain).astype(jnp.bfloat16)
    model_width = tokens.shape[1]
    query_cols = query_weight.shape[1]
    keyval_cols = key_value_weight.shape[1]
    kv_rows = lax.all_gather(key_value_weight, MP_AXES, axis=0, tiled=True)
    pieces = [
        query_weight,
        kv_rows,
        out_weight.T,
        gate_up_weight[0],
    ]
    widths = [piece.shape[1] for piece in pieces]
    sizes = [piece.size for piece in pieces]
    packed_weights = jnp.concatenate([piece.astype(jnp.bfloat16).reshape(-1) for piece in pieces])
    gathered = gather_dp(packed_weights)
    offsets = [0]
    for size in sizes:
        offsets.append(offsets[-1] + size)
    def piece_of(k):
        return gathered[:, offsets[k]:offsets[k + 1]].reshape(model_width, widths[k])
    query_full = piece_of(0)
    keyval_full = piece_of(1)
    out_rows_t = piece_of(2)
    gate_full = piece_of(3)
    ring_pieces = [gate_up_weight[1], down_weight.T]
    ring_size = ring_pieces[0].size
    ring_block = jnp.concatenate([piece.astype(jnp.bfloat16).reshape(-1) for piece in ring_pieces])
    for k, axis in enumerate(DP_AXES):
        ring_block = ring_gather(ring_block, axis, lax.axis_size(axis), k)
    ring_all = ring_block.reshape(data_groups, -1)
    ffn_width = gate_up_weight.shape[2]
    up_relative = ring_all[:, :ring_size].reshape(model_width, ffn_width)
    down_relative_t = ring_all[:, ring_size:].reshape(model_width, ffn_width)
    normed_x = to_relative(normed, axes=("x",))
    queries = fold_rows(normed_x, query_full)
    keyvals = fold_rows(normed_x, keyval_full)
    allowed, cosines, sines = prompt_layout(prompt_lengths[0], row_count, head_dim)
    key_column_width = keyval_cols // 2
    query_heads = rotate_heads(queries, query_gain, cosines, sines).astype(jnp.bfloat16)
    key_head_rows = rotate_heads(keyvals[:, :key_column_width], key_gain, cosines, sines).astype(
        jnp.bfloat16
    )
    value_head_rows = keyvals[:, key_column_width:].astype(jnp.bfloat16)
    cache_rows = jnp.concatenate([key_head_rows, value_head_rows], axis=1)
    pages_here = row_count // PAGE_SLOTS
    cache_pages = cache_rows.reshape(pages_here, PAGE_SLOTS, keyval_cols)
    capacity = pages_here // min(pages_here, data_groups)
    owner = page_table // pages_here
    target = page_table % pages_here
    page_index = jnp.arange(pages_here, dtype=jnp.int32)
    earlier = (owner[None, :] == owner[:, None]) & (page_index[None, :] < page_index[:, None])
    send_slot = owner * capacity + jnp.sum(earlier.astype(jnp.int32), axis=1)
    slot_ids = jnp.arange(data_groups * capacity, dtype=jnp.int32)
    placing = slot_ids[:, None] == send_slot[None, :]
    flat_rows = cache_pages.reshape(pages_here, -1)
    mark_cols = 128
    marks_col = jnp.broadcast_to((target + 1).astype(jnp.bfloat16)[:, None], (pages_here, mark_cols))
    flat_marked = jnp.concatenate([flat_rows, marks_col], axis=1)
    packed = jnp.dot(placing.astype(jnp.bfloat16), flat_marked, preferred_element_type=jnp.float32)
    got_pages = lax.all_to_all(
        packed.astype(jnp.bfloat16).reshape(data_groups, capacity, -1),
        DP_AXES,
        split_axis=0,
        concat_axis=0,
        tiled=True,
    )
    got_flat = got_pages.reshape(data_groups * capacity, -1)
    flat_rows = got_flat[:, : flat_rows.shape[1]]
    got_marks = got_flat[:, flat_rows.shape[1]].astype(jnp.int32)
    choosing = (got_marks[None, :] == page_index[:, None] + 1).astype(jnp.bfloat16)
    kv_pool = (
        jnp.dot(choosing, flat_rows, preferred_element_type=jnp.float32)
        .astype(jnp.bfloat16)
        .reshape(pages_here, PAGE_SLOTS, keyval_cols)
    )
    heads_here = query_cols // head_dim
    shard_portion = QUERY_HEADS // KEYVALUE_HEADS
    kv_heads = key_column_width // head_dim
    global_heads = part_index * heads_here + jnp.arange(heads_here, dtype=jnp.int32)
    source_heads = global_heads // shard_portion
    query_grid = query_heads.reshape(row_count, heads_here, head_dim)
    key_page_grid = jnp.take(
        key_head_rows.reshape(row_count, kv_heads, head_dim), source_heads, axis=1
    )
    value_page_grid = jnp.take(
        value_head_rows.reshape(row_count, kv_heads, head_dim), source_heads, axis=1
    )
    scores = jnp.einsum(
        "qhd,khd->hqk", query_grid, key_page_grid, preferred_element_type=jnp.float32
    ) * head_dim ** (-0.5)
    scores = jnp.where(allowed[None, :, :], scores, -1e30)
    probs = softmax_rows(scores).astype(jnp.bfloat16)
    attended = jnp.einsum(
        "hqk,khd->qhd", probs, value_page_grid, preferred_element_type=jnp.float32
    )
    attended = attended.astype(jnp.bfloat16).reshape(row_count, query_cols)
    attn_part = to_relative(
        jnp.einsum("tr,cr->tc", attended, out_rows_t, preferred_element_type=jnp.float32),
        inverse=True,
        axes=("x",),
    )
    attn_total = lax.psum(attn_part.astype(jnp.bfloat16), MP_AXES).astype(jnp.float32)
    residual_all = inputs_wide + attn_total
    ffn_input = rms_rows(residual_all, ffn_gain).astype(jnp.bfloat16)
    residual_own = lax.dynamic_slice_in_dim(residual_all, part_index * own_rows, own_rows, 0)
    gate = fold_rows(to_relative(ffn_input, axes=("x",)), gate_full)
    upward = fold_rows(to_relative(ffn_input), up_relative)
    hidden = (jax.nn.silu(gate) * upward).astype(jnp.bfloat16)
    down_part = to_relative(
        jnp.einsum("tf,cf->tc", hidden, down_relative_t, preferred_element_type=jnp.float32),
        inverse=True,
    )
    swap = [(0, 1), (1, 0)]
    high = lax.axis_index("yhi")
    half_rows = row_count // 2
    mine_half = lax.dynamic_slice_in_dim(down_part, high * half_rows, half_rows, 0)
    other_half = lax.dynamic_slice_in_dim(down_part, (1 - high) * half_rows, half_rows, 0)
    got_half = lax.ppermute(other_half.astype(jnp.bfloat16), "yhi", swap)
    half_sum = mine_half + got_half.astype(jnp.float32)
    core = lax.axis_index("core")
    mine_rows = lax.dynamic_slice_in_dim(half_sum, core * own_rows, own_rows, 0)
    other_rows = lax.dynamic_slice_in_dim(half_sum, (1 - core) * own_rows, own_rows, 0)
    got_rows = lax.ppermute(other_rows, "core", swap)
    layer_out = (residual_own + (mine_rows + got_rows)).astype(jnp.bfloat16)
    return (layer_out, kv_pool)


def solution(mesh):
    sizes = [mesh.shape["dp"] // (2 * 4), 2, 4, 2, mesh.shape["mp"] // 2]
    fine_mesh = Mesh(mesh.devices.reshape(sizes), DP_AXES + MP_AXES)
    rows = DP_AXES + MP_AXES
    return jax.shard_map(
        per_device,
        mesh=fine_mesh,
        in_specs=(
            P(rows, None),
            P(),
            P(DP_AXES, MP_AXES),
            P(rows, None),
            P(),
            P(),
            P(MP_AXES, DP_AXES),
            P(),
            P(None, DP_AXES, MP_AXES),
            P(MP_AXES, DP_AXES),
            P(DP_AXES, None),
            P(DP_AXES),
        ),
        out_specs=(P(rows, None), P(DP_AXES, None, None)),
        check_vma=False,
    )
```

```python
import jax
import jax.numpy as jnp
from jax import lax
from jax.sharding import Mesh, PartitionSpec as P

QUERY_HEADS = 20
KEYVALUE_HEADS = 5
PAGE_SLOTS = 16


EPSILON = 1e-06


def rms_rows(values, gain):
    scale = lax.rsqrt(jnp.mean(values * values, axis=-1, keepdims=True) + EPSILON)
    return values * scale * gain


def prompt_layout(lengths, row_count, head_dim):
    ends = jnp.cumsum(lengths)
    starts = ends - lengths
    row_index = jnp.arange(row_count, dtype=jnp.int32)
    segment = jnp.sum((row_index[:, None] >= ends[None, :]).astype(jnp.int32), axis=1)
    prompt_ids = jnp.arange(lengths.shape[0], dtype=jnp.int32)
    first_row = jnp.sum(
        jnp.where(segment[:, None] == prompt_ids[None, :], starts[None, :], 0), axis=1
    )
    position = row_index - first_row
    half_dim = head_dim // 2
    frequency = 10000.0 ** (-(jnp.arange(half_dim, dtype=jnp.float32) * (2.0 / head_dim)))
    angle = position.astype(jnp.float32)[:, None] * frequency[None, :]
    allowed = (segment[:, None] == segment[None, :]) & (row_index[None, :] <= row_index[:, None])
    return (allowed, jnp.cos(angle)[:, None, :], jnp.sin(angle)[:, None, :])


def rotate_heads(flat, gain, cosines, sines):
    row_count = flat.shape[0]
    head_dim = gain.shape[0]
    heads = rms_rows(flat.reshape(row_count, -1, head_dim), gain)
    half_dim = head_dim // 2
    first = heads[..., :half_dim]
    second = heads[..., half_dim:]
    turned = jnp.concatenate(
        [first * cosines - second * sines, second * cosines + first * sines], axis=-1
    )
    return turned.reshape(row_count, -1)


def softmax_rows(scores):
    peak = jnp.max(scores, axis=-1, keepdims=True)
    weights = jnp.exp(scores - peak)
    return weights / jnp.sum(weights, axis=-1, keepdims=True)


def fold_rows(left, piece):
    return jnp.dot(left, piece, preferred_element_type=jnp.float32)


DP_AXES = ("z", "ylo", "x")
MP_AXES = ("yhi", "core")


def gather_dp(flat):
    staged = ring_gather(flat, "x", lax.axis_size("x"), 0)
    for axis in ("ylo", "z"):
        staged = lax.all_gather(staged, axis, axis=0, tiled=True)
    return staged


def ring_gather(block, axis, count, at):
    forward_perm = [(i, (i + 1) % count) for i in range(count)]
    backward_perm = [(i, (i - 1) % count) for i in range(count)]
    chunks = {0: block}
    ahead = block
    behind = block
    for step in range(1, count // 2 + 1):
        if count == 2:
            chunks[1] = lax.ppermute(block, axis, forward_perm)
        elif step < count - step:
            ahead = lax.ppermute(ahead, axis, forward_perm)
            behind = lax.ppermute(behind, axis, backward_perm)
            chunks[count - step] = ahead
            chunks[step] = behind
        else:
            half = block.shape[-1] // 2
            first = lax.ppermute(ahead[..., :half], axis, forward_perm)
            second = lax.ppermute(behind[..., half:], axis, backward_perm)
            chunks[step] = jnp.concatenate([first, second], axis=-1)
    return jnp.stack([chunks[r] for r in range(count)], axis=at)


def to_relative(values, inverse=False, axes=DP_AXES):
    lead = values.shape[:-1]
    sizes = [lax.axis_size(axis) for axis in DP_AXES]
    grid = values.reshape(lead + tuple(sizes) + (-1,))
    for k, axis in enumerate(DP_AXES):
        if axis not in axes:
            continue
        shift = lax.axis_index(axis)
        grid = jnp.roll(grid, shift if inverse else -shift, axis=len(lead) + k)
    return grid.reshape(values.shape)


def per_device(
    tokens,
    attn_gain,
    query_weight,
    key_value_weight,
    query_gain,
    key_gain,
    out_weight,
    ffn_gain,
    gate_up_weight,
    down_weight,
    prompt_lengths,
    page_table,
):
    head_dim = query_gain.shape[0]
    data_groups = 1
    for axis in DP_AXES:
        data_groups *= lax.axis_size(axis)
    part_index = lax.axis_index(MP_AXES)
    own_rows = tokens.shape[0]
    group_tokens = lax.all_gather(tokens, MP_AXES, axis=0, tiled=True)
    row_count = group_tokens.shape[0]
    inputs_wide = group_tokens.astype(jnp.float32)
    normed = rms_rows(inputs_wide, attn_gain).astype(jnp.bfloat16)
    model_width = tokens.shape[1]
    query_cols = query_weight.shape[1]
    keyval_cols = key_value_weight.shape[1]
    kv_rows = lax.all_gather(key_value_weight, MP_AXES, axis=0, tiled=True)
    pieces = [
        query_weight,
        out_weight.T,
        gate_up_weight[0],
    ]
    widths = [piece.shape[1] for piece in pieces]
    sizes = [piece.size for piece in pieces]
    packed_weights = jnp.concatenate([piece.astype(jnp.bfloat16).reshape(-1) for piece in pieces])
    gathered = gather_dp(packed_weights)
    offsets = [0]
    for size in sizes:
        offsets.append(offsets[-1] + size)
    def piece_of(k):
        return gathered[:, offsets[k]:offsets[k + 1]].reshape(model_width, widths[k])
    query_full = piece_of(0)
    out_rows_t = piece_of(1)
    gate_full = piece_of(2)
    ring_pieces = [gate_up_weight[1], down_weight.T, kv_rows]
    ring_size = ring_pieces[0].size
    ring_block = jnp.concatenate([piece.astype(jnp.bfloat16).reshape(-1) for piece in ring_pieces])
    for k, axis in enumerate(DP_AXES):
        ring_block = ring_gather(ring_block, axis, lax.axis_size(axis), k)
    ring_all = ring_block.reshape(data_groups, -1)
    ffn_width = gate_up_weight.shape[2]
    up_relative = ring_all[:, :ring_size].reshape(model_width, ffn_width)
    down_relative_t = ring_all[:, ring_size:2 * ring_size].reshape(model_width, ffn_width)
    keyval_relative = ring_all[:, 2 * ring_size:].reshape(model_width, keyval_cols)
    normed_x = to_relative(normed, axes=("x",))
    keyvals = fold_rows(to_relative(normed), keyval_relative)
    allowed, cosines, sines = prompt_layout(prompt_lengths[0], row_count, head_dim)
    key_column_width = keyval_cols // 2
    key_head_rows = rotate_heads(keyvals[:, :key_column_width], key_gain, cosines, sines).astype(
        jnp.bfloat16
    )
    value_head_rows = keyvals[:, key_column_width:].astype(jnp.bfloat16)
    cache_rows = jnp.concatenate([key_head_rows, value_head_rows], axis=1)
    pages_here = row_count // PAGE_SLOTS
    cache_pages = cache_rows.reshape(pages_here, PAGE_SLOTS, keyval_cols)
    capacity = pages_here // min(pages_here, data_groups)
    owner = page_table // pages_here
    target = page_table % pages_here
    page_index = jnp.arange(pages_here, dtype=jnp.int32)
    earlier = (owner[None, :] == owner[:, None]) & (page_index[None, :] < page_index[:, None])
    send_slot = owner * capacity + jnp.sum(earlier.astype(jnp.int32), axis=1)
    slot_ids = jnp.arange(data_groups * capacity, dtype=jnp.int32)
    placing = slot_ids[:, None] == send_slot[None, :]
    flat_rows = cache_pages.reshape(pages_here, -1)
    mark_cols = 128
    marks_col = jnp.broadcast_to((target + 1).astype(jnp.bfloat16)[:, None], (pages_here, mark_cols))
    flat_marked = jnp.concatenate([flat_rows, marks_col], axis=1)
    packed = jnp.dot(placing.astype(jnp.bfloat16), flat_marked, preferred_element_type=jnp.float32)
    got_pages = lax.all_to_all(
        packed.astype(jnp.bfloat16).reshape(data_groups, capacity, -1),
        DP_AXES,
        split_axis=0,
        concat_axis=0,
        tiled=True,
    )
    got_pages, query_full = lax.optimization_barrier((got_pages, query_full))
    queries = fold_rows(normed_x, query_full)
    query_heads = rotate_heads(queries, query_gain, cosines, sines).astype(jnp.bfloat16)
    got_flat = got_pages.reshape(data_groups * capacity, -1)
    flat_rows = got_flat[:, : flat_rows.shape[1]]
    got_marks = got_flat[:, flat_rows.shape[1]].astype(jnp.int32)
    choosing = (got_marks[None, :] == page_index[:, None] + 1).astype(jnp.bfloat16)
    kv_pool = (
        jnp.dot(choosing, flat_rows, preferred_element_type=jnp.float32)
        .astype(jnp.bfloat16)
        .reshape(pages_here, PAGE_SLOTS, keyval_cols)
    )
    heads_here = query_cols // head_dim
    shard_portion = QUERY_HEADS // KEYVALUE_HEADS
    kv_heads = key_column_width // head_dim
    global_heads = part_index * heads_here + jnp.arange(heads_here, dtype=jnp.int32)
    source_heads = global_heads // shard_portion
    query_grid = query_heads.reshape(row_count, heads_here, head_dim)
    key_page_grid = jnp.take(
        key_head_rows.reshape(row_count, kv_heads, head_dim), source_heads, axis=1
    )
    value_page_grid = jnp.take(
        value_head_rows.reshape(row_count, kv_heads, head_dim), source_heads, axis=1
    )
    scores = jnp.einsum(
        "qhd,khd->hqk", query_grid, key_page_grid, preferred_element_type=jnp.float32
    ) * head_dim ** (-0.5)
    scores = jnp.where(allowed[None, :, :], scores, -1e30)
    probs = softmax_rows(scores).astype(jnp.bfloat16)
    attended = jnp.einsum(
        "hqk,khd->qhd", probs, value_page_grid, preferred_element_type=jnp.float32
    )
    attended = attended.astype(jnp.bfloat16).reshape(row_count, query_cols)
    attn_part = to_relative(
        jnp.einsum("tr,cr->tc", attended, out_rows_t, preferred_element_type=jnp.float32),
        inverse=True,
        axes=("x",),
    )
    attn_total = lax.psum(attn_part.astype(jnp.bfloat16), MP_AXES).astype(jnp.float32)
    residual_all = inputs_wide + attn_total
    ffn_input = rms_rows(residual_all, ffn_gain).astype(jnp.bfloat16)
    residual_own = lax.dynamic_slice_in_dim(residual_all, part_index * own_rows, own_rows, 0)
    gate = fold_rows(to_relative(ffn_input, axes=("x",)), gate_full)
    upward = fold_rows(to_relative(ffn_input), up_relative)
    hidden = (jax.nn.silu(gate) * upward).astype(jnp.bfloat16)
    down_part = to_relative(
        jnp.einsum("tf,cf->tc", hidden, down_relative_t, preferred_element_type=jnp.float32),
        inverse=True,
    )
    swap = [(0, 1), (1, 0)]
    high = lax.axis_index("yhi")
    half_rows = row_count // 2
    mine_half = lax.dynamic_slice_in_dim(down_part, high * half_rows, half_rows, 0)
    other_half = lax.dynamic_slice_in_dim(down_part, (1 - high) * half_rows, half_rows, 0)
    got_half = lax.ppermute(other_half.astype(jnp.bfloat16), "yhi", swap)
    half_sum = mine_half + got_half.astype(jnp.float32)
    core = lax.axis_index("core")
    mine_rows = lax.dynamic_slice_in_dim(half_sum, core * own_rows, own_rows, 0)
    other_rows = lax.dynamic_slice_in_dim(half_sum, (1 - core) * own_rows, own_rows, 0)
    got_rows = lax.ppermute(other_rows, "core", swap)
    layer_out = (residual_own + (mine_rows + got_rows)).astype(jnp.bfloat16)
    return (layer_out, kv_pool)


def solution(mesh):
    sizes = [mesh.shape["dp"] // (2 * 4), 2, 4, 2, mesh.shape["mp"] // 2]
    fine_mesh = Mesh(mesh.devices.reshape(sizes), DP_AXES + MP_AXES)
    rows = DP_AXES + MP_AXES
    return jax.shard_map(
        per_device,
        mesh=fine_mesh,
        in_specs=(
            P(rows, None),
            P(),
            P(DP_AXES, MP_AXES),
            P(rows, None),
            P(),
            P(),
            P(MP_AXES, DP_AXES),
            P(),
            P(None, DP_AXES, MP_AXES),
            P(MP_AXES, DP_AXES),
            P(DP_AXES, None),
            P(DP_AXES),
        ),
        out_specs=(P(rows, None), P(DP_AXES, None, None)),
        check_vma=False,
    )
```

```python
import jax
import jax.numpy as jnp
from jax import lax
from jax.sharding import Mesh, PartitionSpec as P

QUERY_HEADS = 20
KEYVALUE_HEADS = 5
PAGE_SLOTS = 16


EPSILON = 1e-06


def rms_rows(values, gain):
    scale = lax.rsqrt(jnp.mean(values * values, axis=-1, keepdims=True) + EPSILON)
    return values * scale * gain


def prompt_layout(lengths, row_count, head_dim):
    ends = jnp.cumsum(lengths)
    starts = ends - lengths
    row_index = jnp.arange(row_count, dtype=jnp.int32)
    segment = jnp.sum((row_index[:, None] >= ends[None, :]).astype(jnp.int32), axis=1)
    prompt_ids = jnp.arange(lengths.shape[0], dtype=jnp.int32)
    first_row = jnp.sum(
        jnp.where(segment[:, None] == prompt_ids[None, :], starts[None, :], 0), axis=1
    )
    position = row_index - first_row
    half_dim = head_dim // 2
    frequency = 10000.0 ** (-(jnp.arange(half_dim, dtype=jnp.float32) * (2.0 / head_dim)))
    angle = position.astype(jnp.float32)[:, None] * frequency[None, :]
    allowed = (segment[:, None] == segment[None, :]) & (row_index[None, :] <= row_index[:, None])
    return (allowed, jnp.cos(angle)[:, None, :], jnp.sin(angle)[:, None, :])


def rotate_heads(flat, gain, cosines, sines):
    row_count = flat.shape[0]
    head_dim = gain.shape[0]
    heads = rms_rows(flat.reshape(row_count, -1, head_dim), gain)
    half_dim = head_dim // 2
    first = heads[..., :half_dim]
    second = heads[..., half_dim:]
    turned = jnp.concatenate(
        [first * cosines - second * sines, second * cosines + first * sines], axis=-1
    )
    return turned.reshape(row_count, -1)


def softmax_rows(scores):
    peak = jnp.max(scores, axis=-1, keepdims=True)
    weights = jnp.exp(scores - peak)
    return weights / jnp.sum(weights, axis=-1, keepdims=True)


def fold_rows(left, piece):
    return jnp.dot(left, piece, preferred_element_type=jnp.float32)


DP_AXES = ("z", "ylo", "x")
MP_AXES = ("yhi", "core")


def gather_dp(flat):
    staged = ring_gather(flat, "x", lax.axis_size("x"), 0)
    for axis in ("ylo", "z"):
        staged = lax.all_gather(staged, axis, axis=0, tiled=True)
    return staged


def ring_gather(block, axis, count, at):
    forward_perm = [(i, (i + 1) % count) for i in range(count)]
    backward_perm = [(i, (i - 1) % count) for i in range(count)]
    chunks = {0: block}
    ahead = block
    behind = block
    for step in range(1, count // 2 + 1):
        if count == 2:
            chunks[1] = lax.ppermute(block, axis, forward_perm)
        elif step < count - step:
            ahead = lax.ppermute(ahead, axis, forward_perm)
            behind = lax.ppermute(behind, axis, backward_perm)
            chunks[count - step] = ahead
            chunks[step] = behind
        else:
            half = block.shape[-1] // 2
            first = lax.ppermute(ahead[..., :half], axis, forward_perm)
            second = lax.ppermute(behind[..., half:], axis, backward_perm)
            chunks[step] = jnp.concatenate([first, second], axis=-1)
    return jnp.stack([chunks[r] for r in range(count)], axis=at)


def to_relative(values, inverse=False, axes=DP_AXES):
    lead = values.shape[:-1]
    sizes = [lax.axis_size(axis) for axis in DP_AXES]
    grid = values.reshape(lead + tuple(sizes) + (-1,))
    for k, axis in enumerate(DP_AXES):
        if axis not in axes:
            continue
        shift = lax.axis_index(axis)
        grid = jnp.roll(grid, shift if inverse else -shift, axis=len(lead) + k)
    return grid.reshape(values.shape)


def per_device(
    tokens,
    attn_gain,
    query_weight,
    key_value_weight,
    query_gain,
    key_gain,
    out_weight,
    ffn_gain,
    gate_up_weight,
    down_weight,
    prompt_lengths,
    page_table,
):
    head_dim = query_gain.shape[0]
    data_groups = 1
    for axis in DP_AXES:
        data_groups *= lax.axis_size(axis)
    part_index = lax.axis_index(MP_AXES)
    own_rows = tokens.shape[0]
    group_tokens = lax.all_gather(tokens, MP_AXES, axis=0, tiled=True)
    row_count = group_tokens.shape[0]
    inputs_wide = group_tokens.astype(jnp.float32)
    normed = rms_rows(inputs_wide, attn_gain).astype(jnp.bfloat16)
    model_width = tokens.shape[1]
    query_cols = query_weight.shape[1]
    keyval_cols = key_value_weight.shape[1]
    kv_rows = lax.all_gather(key_value_weight, MP_AXES, axis=0, tiled=True)
    pieces = [
        query_weight,
        kv_rows,
        out_weight.T,
        gate_up_weight[0],
    ]
    widths = [piece.shape[1] for piece in pieces]
    sizes = [piece.size for piece in pieces]
    packed_weights = jnp.concatenate([piece.astype(jnp.bfloat16).reshape(-1) for piece in pieces])
    gathered = gather_dp(packed_weights)
    offsets = [0]
    for size in sizes:
        offsets.append(offsets[-1] + size)
    def piece_of(k):
        return gathered[:, offsets[k]:offsets[k + 1]].reshape(model_width, widths[k])
    query_full = piece_of(0)
    keyval_full = piece_of(1)
    out_rows_t = piece_of(2)
    gate_full = piece_of(3)
    ring_pieces = [gate_up_weight[1], down_weight.T]
    ring_size = ring_pieces[0].size
    ring_block = jnp.concatenate([piece.astype(jnp.bfloat16).reshape(-1) for piece in ring_pieces])
    for k, axis in enumerate(DP_AXES):
        ring_block = ring_gather(ring_block, axis, lax.axis_size(axis), k)
    ring_all = ring_block.reshape(data_groups, -1)
    ffn_width = gate_up_weight.shape[2]
    up_relative = ring_all[:, :ring_size].reshape(model_width, ffn_width)
    down_relative_t = ring_all[:, ring_size:].reshape(model_width, ffn_width)
    normed_x = to_relative(normed, axes=("x",))
    queries = fold_rows(normed_x, query_full)
    keyvals = fold_rows(normed_x, keyval_full)
    allowed, cosines, sines = prompt_layout(prompt_lengths[0], row_count, head_dim)
    key_column_width = keyval_cols // 2
    query_heads = rotate_heads(queries, query_gain, cosines, sines).astype(jnp.bfloat16)
    key_head_rows = rotate_heads(keyvals[:, :key_column_width], key_gain, cosines, sines).astype(
        jnp.bfloat16
    )
    value_head_rows = keyvals[:, key_column_width:].astype(jnp.bfloat16)
    cache_rows = jnp.concatenate([key_head_rows, value_head_rows], axis=1)
    pages_here = row_count // PAGE_SLOTS
    cache_pages = cache_rows.reshape(pages_here, PAGE_SLOTS, keyval_cols)
    capacity = pages_here // min(pages_here, data_groups)
    owner = page_table // pages_here
    target = page_table % pages_here
    page_index = jnp.arange(pages_here, dtype=jnp.int32)
    earlier = (owner[None, :] == owner[:, None]) & (page_index[None, :] < page_index[:, None])
    send_slot = owner * capacity + jnp.sum(earlier.astype(jnp.int32), axis=1)
    slot_ids = jnp.arange(data_groups * capacity, dtype=jnp.int32)
    placing = slot_ids[:, None] == send_slot[None, :]
    flat_rows = cache_pages.reshape(pages_here, -1)
    mark_cols = 128
    marks_col = jnp.broadcast_to((target + 1).astype(jnp.bfloat16)[:, None], (pages_here, mark_cols))
    flat_marked = jnp.concatenate([flat_rows, marks_col], axis=1)
    packed = jnp.dot(placing.astype(jnp.bfloat16), flat_marked, preferred_element_type=jnp.float32)
    got_pages = lax.all_to_all(
        packed.astype(jnp.bfloat16).reshape(data_groups, capacity, -1),
        DP_AXES,
        split_axis=0,
        concat_axis=0,
        tiled=True,
    )
    got_flat = got_pages.reshape(data_groups * capacity, -1)
    flat_rows = got_flat[:, : flat_rows.shape[1]]
    got_marks = got_flat[:, flat_rows.shape[1]].astype(jnp.int32)
    choosing = (got_marks[None, :] == page_index[:, None] + 1).astype(jnp.bfloat16)
    kv_pool = (
        jnp.dot(choosing, flat_rows, preferred_element_type=jnp.float32)
        .astype(jnp.bfloat16)
        .reshape(pages_here, PAGE_SLOTS, keyval_cols)
    )
    heads_here = query_cols // head_dim
    shard_portion = QUERY_HEADS // KEYVALUE_HEADS
    kv_heads = key_column_width // head_dim
    global_heads = part_index * heads_here + jnp.arange(heads_here, dtype=jnp.int32)
    source_heads = global_heads // shard_portion
    query_grid = query_heads.reshape(row_count, heads_here, head_dim)
    key_page_grid = jnp.take(
        key_head_rows.reshape(row_count, kv_heads, head_dim), source_heads, axis=1
    )
    value_page_grid = jnp.take(
        value_head_rows.reshape(row_count, kv_heads, head_dim), source_heads, axis=1
    )
    scores = jnp.einsum(
        "qhd,khd->hqk", query_grid, key_page_grid, preferred_element_type=jnp.float32
    ) * head_dim ** (-0.5)
    scores = jnp.where(allowed[None, :, :], scores, -1e30)
    probs = softmax_rows(scores).astype(jnp.bfloat16)
    attended = jnp.einsum(
        "hqk,khd->qhd", probs, value_page_grid, preferred_element_type=jnp.float32
    )
    attended = attended.astype(jnp.bfloat16).reshape(row_count, query_cols)
    attn_part = to_relative(
        jnp.einsum("tr,cr->tc", attended, out_rows_t, preferred_element_type=jnp.float32),
        inverse=True,
        axes=("x",),
    )
    attn_total = lax.psum(attn_part.astype(jnp.bfloat16), MP_AXES).astype(jnp.float32)
    residual_all = inputs_wide + attn_total
    ffn_input = rms_rows(residual_all, ffn_gain).astype(jnp.bfloat16)
    kv_pool, ffn_input = lax.optimization_barrier((kv_pool, ffn_input))
    residual_own = lax.dynamic_slice_in_dim(residual_all, part_index * own_rows, own_rows, 0)
    gate = fold_rows(to_relative(ffn_input, axes=("x",)), gate_full)
    upward = fold_rows(to_relative(ffn_input), up_relative)
    hidden = (jax.nn.silu(gate) * upward).astype(jnp.bfloat16)
    down_part = to_relative(
        jnp.einsum("tf,cf->tc", hidden, down_relative_t, preferred_element_type=jnp.float32),
        inverse=True,
    )
    swap = [(0, 1), (1, 0)]
    high = lax.axis_index("yhi")
    half_rows = row_count // 2
    mine_half = lax.dynamic_slice_in_dim(down_part, high * half_rows, half_rows, 0)
    other_half = lax.dynamic_slice_in_dim(down_part, (1 - high) * half_rows, half_rows, 0)
    got_half = lax.ppermute(other_half.astype(jnp.bfloat16), "yhi", swap)
    half_sum = mine_half + got_half.astype(jnp.float32)
    core = lax.axis_index("core")
    mine_rows = lax.dynamic_slice_in_dim(half_sum, core * own_rows, own_rows, 0)
    other_rows = lax.dynamic_slice_in_dim(half_sum, (1 - core) * own_rows, own_rows, 0)
    got_rows = lax.ppermute(other_rows, "core", swap)
    layer_out = (residual_own + (mine_rows + got_rows)).astype(jnp.bfloat16)
    return (layer_out, kv_pool)


def solution(mesh):
    sizes = [mesh.shape["dp"] // (2 * 4), 2, 4, 2, mesh.shape["mp"] // 2]
    fine_mesh = Mesh(mesh.devices.reshape(sizes), DP_AXES + MP_AXES)
    rows = DP_AXES + MP_AXES
    return jax.shard_map(
        per_device,
        mesh=fine_mesh,
        in_specs=(
            P(rows, None),
            P(),
            P(DP_AXES, MP_AXES),
            P(rows, None),
            P(),
            P(),
            P(MP_AXES, DP_AXES),
            P(),
            P(None, DP_AXES, MP_AXES),
            P(MP_AXES, DP_AXES),
            P(DP_AXES, None),
            P(DP_AXES),
        ),
        out_specs=(P(rows, None), P(DP_AXES, None, None)),
        check_vma=False,
    )
```

```python
import jax
import jax.numpy as jnp
from jax import lax
from jax.sharding import Mesh, PartitionSpec as P

QUERY_HEADS = 20
KEYVALUE_HEADS = 5
PAGE_SLOTS = 16


EPSILON = 1e-06


def rms_rows(values, gain):
    scale = lax.rsqrt(jnp.mean(values * values, axis=-1, keepdims=True) + EPSILON)
    return values * scale * gain


def prompt_layout(lengths, row_count, head_dim):
    ends = jnp.cumsum(lengths)
    starts = ends - lengths
    row_index = jnp.arange(row_count, dtype=jnp.int32)
    segment = jnp.sum((row_index[:, None] >= ends[None, :]).astype(jnp.int32), axis=1)
    prompt_ids = jnp.arange(lengths.shape[0], dtype=jnp.int32)
    first_row = jnp.sum(
        jnp.where(segment[:, None] == prompt_ids[None, :], starts[None, :], 0), axis=1
    )
    position = row_index - first_row
    half_dim = head_dim // 2
    frequency = 10000.0 ** (-(jnp.arange(half_dim, dtype=jnp.float32) * (2.0 / head_dim)))
    angle = position.astype(jnp.float32)[:, None] * frequency[None, :]
    allowed = (segment[:, None] == segment[None, :]) & (row_index[None, :] <= row_index[:, None])
    return (allowed, jnp.cos(angle)[:, None, :], jnp.sin(angle)[:, None, :])


def rotate_heads(flat, gain, cosines, sines):
    row_count = flat.shape[0]
    head_dim = gain.shape[0]
    heads = rms_rows(flat.reshape(row_count, -1, head_dim), gain)
    half_dim = head_dim // 2
    first = heads[..., :half_dim]
    second = heads[..., half_dim:]
    turned = jnp.concatenate(
        [first * cosines - second * sines, second * cosines + first * sines], axis=-1
    )
    return turned.reshape(row_count, -1)


def softmax_rows(scores):
    peak = jnp.max(scores, axis=-1, keepdims=True)
    weights = jnp.exp(scores - peak)
    return weights / jnp.sum(weights, axis=-1, keepdims=True)


def fold_rows(left, piece):
    return jnp.dot(left, piece, preferred_element_type=jnp.float32)


DP_AXES = ("z", "ylo", "x")
MP_AXES = ("yhi", "core")


def gather_dp(flat):
    staged = ring_gather(flat, "x", lax.axis_size("x"), 0)
    for axis in ("ylo", "z"):
        staged = lax.all_gather(staged, axis, axis=0, tiled=True)
    return staged


def ring_gather(block, axis, count, at):
    forward_perm = [(i, (i + 1) % count) for i in range(count)]
    backward_perm = [(i, (i - 1) % count) for i in range(count)]
    chunks = {0: block}
    ahead = block
    behind = block
    for step in range(1, count // 2 + 1):
        if count == 2:
            chunks[1] = lax.ppermute(block, axis, forward_perm)
        elif step < count - step:
            ahead = lax.ppermute(ahead, axis, forward_perm)
            behind = lax.ppermute(behind, axis, backward_perm)
            chunks[count - step] = ahead
            chunks[step] = behind
        else:
            half = block.shape[-1] // 2
            first = lax.ppermute(ahead[..., :half], axis, forward_perm)
            second = lax.ppermute(behind[..., half:], axis, backward_perm)
            chunks[step] = jnp.concatenate([first, second], axis=-1)
    return jnp.stack([chunks[r] for r in range(count)], axis=at)


def to_relative(values, inverse=False, axes=DP_AXES):
    lead = values.shape[:-1]
    sizes = [lax.axis_size(axis) for axis in DP_AXES]
    grid = values.reshape(lead + tuple(sizes) + (-1,))
    for k, axis in enumerate(DP_AXES):
        if axis not in axes:
            continue
        shift = lax.axis_index(axis)
        grid = jnp.roll(grid, shift if inverse else -shift, axis=len(lead) + k)
    return grid.reshape(values.shape)


def per_device(
    tokens,
    attn_gain,
    query_weight,
    key_value_weight,
    query_gain,
    key_gain,
    out_weight,
    ffn_gain,
    gate_up_weight,
    down_weight,
    prompt_lengths,
    page_table,
):
    head_dim = query_gain.shape[0]
    data_groups = 1
    for axis in DP_AXES:
        data_groups *= lax.axis_size(axis)
    part_index = lax.axis_index(MP_AXES)
    own_rows = tokens.shape[0]
    group_tokens = lax.all_gather(tokens, MP_AXES, axis=0, tiled=True)
    row_count = group_tokens.shape[0]
    inputs_wide = group_tokens.astype(jnp.float32)
    normed = rms_rows(inputs_wide, attn_gain).astype(jnp.bfloat16)
    model_width = tokens.shape[1]
    query_cols = query_weight.shape[1]
    keyval_cols = key_value_weight.shape[1]
    kv_rows = lax.all_gather(key_value_weight, MP_AXES, axis=0, tiled=True)
    pieces = [
        query_weight,
        kv_rows,
        out_weight.T,
        gate_up_weight[0],
    ]
    widths = [piece.shape[1] for piece in pieces]
    sizes = [piece.size for piece in pieces]
    packed_weights = jnp.concatenate([piece.astype(jnp.bfloat16).reshape(-1) for piece in pieces])
    gathered = gather_dp(packed_weights)
    offsets = [0]
    for size in sizes:
        offsets.append(offsets[-1] + size)
    def piece_of(k):
        return gathered[:, offsets[k]:offsets[k + 1]].reshape(model_width, widths[k])
    query_full = piece_of(0)
    keyval_full = piece_of(1)
    out_rows_t = piece_of(2)
    gate_full = piece_of(3)
    ring_pieces = [gate_up_weight[1], down_weight.T]
    ring_size = ring_pieces[0].size
    ring_block = jnp.concatenate([piece.astype(jnp.bfloat16).reshape(-1) for piece in ring_pieces])
    for k, axis in enumerate(DP_AXES):
        ring_block = ring_gather(ring_block, axis, lax.axis_size(axis), k)
    ring_all = ring_block.reshape(data_groups, -1)
    ffn_width = gate_up_weight.shape[2]
    up_relative = ring_all[:, :ring_size].reshape(model_width, ffn_width)
    down_relative_t = ring_all[:, ring_size:].reshape(model_width, ffn_width)
    normed_x = to_relative(normed, axes=("x",))
    queries = fold_rows(normed_x, query_full)
    keyvals = fold_rows(normed_x, keyval_full)
    allowed, cosines, sines = prompt_layout(prompt_lengths[0], row_count, head_dim)
    key_column_width = keyval_cols // 2
    query_heads = rotate_heads(queries, query_gain, cosines, sines).astype(jnp.bfloat16)
    key_head_rows = rotate_heads(keyvals[:, :key_column_width], key_gain, cosines, sines).astype(
        jnp.bfloat16
    )
    value_head_rows = keyvals[:, key_column_width:].astype(jnp.bfloat16)
    cache_rows = jnp.concatenate([key_head_rows, value_head_rows], axis=1)
    pages_here = row_count // PAGE_SLOTS
    cache_pages = cache_rows.reshape(pages_here, PAGE_SLOTS, keyval_cols)
    capacity = pages_here // min(pages_here, data_groups)
    owner = page_table // pages_here
    target = page_table % pages_here
    page_index = jnp.arange(pages_here, dtype=jnp.int32)
    earlier = (owner[None, :] == owner[:, None]) & (page_index[None, :] < page_index[:, None])
    send_slot = owner * capacity + jnp.sum(earlier.astype(jnp.int32), axis=1)
    slot_ids = jnp.arange(data_groups * capacity, dtype=jnp.int32)
    placing = slot_ids[:, None] == send_slot[None, :]
    mp_count = lax.axis_size(MP_AXES)
    slot_share = PAGE_SLOTS // mp_count
    my_slots = lax.dynamic_slice_in_dim(cache_pages, part_index * slot_share, slot_share, 1)
    flat_rows = my_slots.reshape(pages_here, -1)
    mark_cols = 128
    marks_col = jnp.broadcast_to((target + 1).astype(jnp.bfloat16)[:, None], (pages_here, mark_cols))
    flat_marked = jnp.concatenate([flat_rows, marks_col], axis=1)
    packed = jnp.dot(placing.astype(jnp.bfloat16), flat_marked, preferred_element_type=jnp.float32)
    got_pages = lax.all_to_all(
        packed.astype(jnp.bfloat16).reshape(data_groups, capacity, -1),
        DP_AXES,
        split_axis=0,
        concat_axis=0,
        tiled=True,
    )
    got_flat = got_pages.reshape(data_groups * capacity, -1)
    flat_rows = got_flat[:, : flat_rows.shape[1]]
    got_marks = got_flat[:, flat_rows.shape[1]].astype(jnp.int32)
    choosing = (got_marks[None, :] == page_index[:, None] + 1).astype(jnp.bfloat16)
    pool_part = (
        jnp.dot(choosing, flat_rows, preferred_element_type=jnp.float32)
        .astype(jnp.bfloat16)
        .reshape(1, pages_here, slot_share, keyval_cols)
    )
    pool_parts = lax.all_gather(pool_part, MP_AXES, axis=0, tiled=True)
    kv_pool = jnp.transpose(pool_parts, (1, 0, 2, 3)).reshape(pages_here, PAGE_SLOTS, keyval_cols)
    heads_here = query_cols // head_dim
    shard_portion = QUERY_HEADS // KEYVALUE_HEADS
    kv_heads = key_column_width // head_dim
    global_heads = part_index * heads_here + jnp.arange(heads_here, dtype=jnp.int32)
    source_heads = global_heads // shard_portion
    query_grid = query_heads.reshape(row_count, heads_here, head_dim)
    key_page_grid = jnp.take(
        key_head_rows.reshape(row_count, kv_heads, head_dim), source_heads, axis=1
    )
    value_page_grid = jnp.take(
        value_head_rows.reshape(row_count, kv_heads, head_dim), source_heads, axis=1
    )
    scores = jnp.einsum(
        "qhd,khd->hqk", query_grid, key_page_grid, preferred_element_type=jnp.float32
    ) * head_dim ** (-0.5)
    scores = jnp.where(allowed[None, :, :], scores, -1e30)
    probs = softmax_rows(scores).astype(jnp.bfloat16)
    attended = jnp.einsum(
        "hqk,khd->qhd", probs, value_page_grid, preferred_element_type=jnp.float32
    )
    attended = attended.astype(jnp.bfloat16).reshape(row_count, query_cols)
    attn_part = to_relative(
        jnp.einsum("tr,cr->tc", attended, out_rows_t, preferred_element_type=jnp.float32),
        inverse=True,
        axes=("x",),
    )
    attn_total = lax.psum(attn_part.astype(jnp.bfloat16), MP_AXES).astype(jnp.float32)
    residual_all = inputs_wide + attn_total
    ffn_input = rms_rows(residual_all, ffn_gain).astype(jnp.bfloat16)
    residual_own = lax.dynamic_slice_in_dim(residual_all, part_index * own_rows, own_rows, 0)
    gate = fold_rows(to_relative(ffn_input, axes=("x",)), gate_full)
    upward = fold_rows(to_relative(ffn_input), up_relative)
    hidden = (jax.nn.silu(gate) * upward).astype(jnp.bfloat16)
    down_part = to_relative(
        jnp.einsum("tf,cf->tc", hidden, down_relative_t, preferred_element_type=jnp.float32),
        inverse=True,
    )
    swap = [(0, 1), (1, 0)]
    high = lax.axis_index("yhi")
    half_rows = row_count // 2
    mine_half = lax.dynamic_slice_in_dim(down_part, high * half_rows, half_rows, 0)
    other_half = lax.dynamic_slice_in_dim(down_part, (1 - high) * half_rows, half_rows, 0)
    got_half = lax.ppermute(other_half.astype(jnp.bfloat16), "yhi", swap)
    half_sum = mine_half + got_half.astype(jnp.float32)
    core = lax.axis_index("core")
    mine_rows = lax.dynamic_slice_in_dim(half_sum, core * own_rows, own_rows, 0)
    other_rows = lax.dynamic_slice_in_dim(half_sum, (1 - core) * own_rows, own_rows, 0)
    got_rows = lax.ppermute(other_rows, "core", swap)
    layer_out = (residual_own + (mine_rows + got_rows)).astype(jnp.bfloat16)
    return (layer_out, kv_pool)


def solution(mesh):
    sizes = [mesh.shape["dp"] // (2 * 4), 2, 4, 2, mesh.shape["mp"] // 2]
    fine_mesh = Mesh(mesh.devices.reshape(sizes), DP_AXES + MP_AXES)
    rows = DP_AXES + MP_AXES
    return jax.shard_map(
        per_device,
        mesh=fine_mesh,
        in_specs=(
            P(rows, None),
            P(),
            P(DP_AXES, MP_AXES),
            P(rows, None),
            P(),
            P(),
            P(MP_AXES, DP_AXES),
            P(),
            P(None, DP_AXES, MP_AXES),
            P(MP_AXES, DP_AXES),
            P(DP_AXES, None),
            P(DP_AXES),
        ),
        out_specs=(P(rows, None), P(DP_AXES, None, None)),
        check_vma=False,
    )
```

```python
import jax
import jax.numpy as jnp
from jax import lax
from jax.sharding import Mesh, PartitionSpec as P

QUERY_HEADS = 20
KEYVALUE_HEADS = 5
PAGE_SLOTS = 16


EPSILON = 1e-06


def rms_rows(values, gain):
    scale = lax.rsqrt(jnp.mean(values * values, axis=-1, keepdims=True) + EPSILON)
    return values * scale * gain


def prompt_layout(lengths, row_count, head_dim):
    ends = jnp.cumsum(lengths)
    starts = ends - lengths
    row_index = jnp.arange(row_count, dtype=jnp.int32)
    segment = jnp.sum((row_index[:, None] >= ends[None, :]).astype(jnp.int32), axis=1)
    prompt_ids = jnp.arange(lengths.shape[0], dtype=jnp.int32)
    first_row = jnp.sum(
        jnp.where(segment[:, None] == prompt_ids[None, :], starts[None, :], 0), axis=1
    )
    position = row_index - first_row
    half_dim = head_dim // 2
    frequency = 10000.0 ** (-(jnp.arange(half_dim, dtype=jnp.float32) * (2.0 / head_dim)))
    angle = position.astype(jnp.float32)[:, None] * frequency[None, :]
    allowed = (segment[:, None] == segment[None, :]) & (row_index[None, :] <= row_index[:, None])
    return (allowed, jnp.cos(angle)[:, None, :], jnp.sin(angle)[:, None, :])


def rotate_heads(flat, gain, cosines, sines):
    row_count = flat.shape[0]
    head_dim = gain.shape[0]
    heads = rms_rows(flat.reshape(row_count, -1, head_dim), gain)
    half_dim = head_dim // 2
    first = heads[..., :half_dim]
    second = heads[..., half_dim:]
    turned = jnp.concatenate(
        [first * cosines - second * sines, second * cosines + first * sines], axis=-1
    )
    return turned.reshape(row_count, -1)


def softmax_rows(scores):
    peak = jnp.max(scores, axis=-1, keepdims=True)
    weights = jnp.exp(scores - peak)
    return weights / jnp.sum(weights, axis=-1, keepdims=True)


def fold_rows(left, piece):
    return jnp.dot(left, piece, preferred_element_type=jnp.float32)


DP_AXES = ("z", "ylo", "x")
MP_AXES = ("yhi", "core")


def gather_dp(flat):
    staged = ring_gather(flat, "x", lax.axis_size("x"), 0)
    for axis in ("ylo", "z"):
        staged = lax.all_gather(staged, axis, axis=0, tiled=True)
    return staged


def ring_gather(block, axis, count, at):
    forward_perm = [(i, (i + 1) % count) for i in range(count)]
    backward_perm = [(i, (i - 1) % count) for i in range(count)]
    chunks = {0: block}
    ahead = block
    behind = block
    for step in range(1, count // 2 + 1):
        if count == 2:
            chunks[1] = lax.ppermute(block, axis, forward_perm)
        elif step < count - step:
            ahead = lax.ppermute(ahead, axis, forward_perm)
            behind = lax.ppermute(behind, axis, backward_perm)
            chunks[count - step] = ahead
            chunks[step] = behind
        else:
            half = block.shape[-1] // 2
            first = lax.ppermute(ahead[..., :half], axis, forward_perm)
            second = lax.ppermute(behind[..., half:], axis, backward_perm)
            chunks[step] = jnp.concatenate([first, second], axis=-1)
    return jnp.stack([chunks[r] for r in range(count)], axis=at)


def to_relative(values, inverse=False, axes=DP_AXES):
    lead = values.shape[:-1]
    sizes = [lax.axis_size(axis) for axis in DP_AXES]
    grid = values.reshape(lead + tuple(sizes) + (-1,))
    for k, axis in enumerate(DP_AXES):
        if axis not in axes:
            continue
        shift = lax.axis_index(axis)
        grid = jnp.roll(grid, shift if inverse else -shift, axis=len(lead) + k)
    return grid.reshape(values.shape)


def per_device(
    tokens,
    attn_gain,
    query_weight,
    key_value_weight,
    query_gain,
    key_gain,
    out_weight,
    ffn_gain,
    gate_up_weight,
    down_weight,
    prompt_lengths,
    page_table,
):
    head_dim = query_gain.shape[0]
    data_groups = 1
    for axis in DP_AXES:
        data_groups *= lax.axis_size(axis)
    part_index = lax.axis_index(MP_AXES)
    own_rows = tokens.shape[0]
    group_tokens = lax.all_gather(tokens, MP_AXES, axis=0, tiled=True)
    row_count = group_tokens.shape[0]
    inputs_wide = group_tokens.astype(jnp.float32)
    normed = rms_rows(inputs_wide, attn_gain).astype(jnp.bfloat16)
    model_width = tokens.shape[1]
    query_cols = query_weight.shape[1]
    keyval_cols = key_value_weight.shape[1]
    kv_rows = lax.all_gather(key_value_weight, MP_AXES, axis=0, tiled=True)
    pieces = [
        query_weight,
        kv_rows,
        out_weight.T,
        gate_up_weight[0],
    ]
    widths = [piece.shape[1] for piece in pieces]
    sizes = [piece.size for piece in pieces]
    packed_weights = jnp.concatenate([piece.astype(jnp.bfloat16).reshape(-1) for piece in pieces])
    gathered = gather_dp(packed_weights)
    offsets = [0]
    for size in sizes:
        offsets.append(offsets[-1] + size)
    def piece_of(k):
        return gathered[:, offsets[k]:offsets[k + 1]].reshape(model_width, widths[k])
    query_full = piece_of(0)
    keyval_full = piece_of(1)
    out_rows_t = piece_of(2)
    gate_full = piece_of(3)
    ring_pieces = [gate_up_weight[1], down_weight.T]
    ring_size = ring_pieces[0].size
    ring_block = jnp.concatenate([piece.astype(jnp.bfloat16).reshape(-1) for piece in ring_pieces])
    for k, axis in enumerate(DP_AXES):
        ring_block = ring_gather(ring_block, axis, lax.axis_size(axis), k)
    ring_all = ring_block.reshape(data_groups, -1)
    ffn_width = gate_up_weight.shape[2]
    up_relative = ring_all[:, :ring_size].reshape(model_width, ffn_width)
    down_relative_t = ring_all[:, ring_size:].reshape(model_width, ffn_width)
    normed_x = to_relative(normed, axes=("x",))
    queries = fold_rows(normed_x, query_full)
    keyvals = fold_rows(normed_x, keyval_full)
    allowed, cosines, sines = prompt_layout(prompt_lengths[0], row_count, head_dim)
    key_column_width = keyval_cols // 2
    query_heads = rotate_heads(queries, query_gain, cosines, sines).astype(jnp.bfloat16)
    key_head_rows = rotate_heads(keyvals[:, :key_column_width], key_gain, cosines, sines).astype(
        jnp.bfloat16
    )
    value_head_rows = keyvals[:, key_column_width:].astype(jnp.bfloat16)
    cache_rows = jnp.concatenate([key_head_rows, value_head_rows], axis=1)
    pages_here = row_count // PAGE_SLOTS
    cache_pages = cache_rows.reshape(pages_here, PAGE_SLOTS, keyval_cols)
    capacity = pages_here // min(pages_here, data_groups)
    owner = page_table // pages_here
    target = page_table % pages_here
    page_index = jnp.arange(pages_here, dtype=jnp.int32)
    earlier = (owner[None, :] == owner[:, None]) & (page_index[None, :] < page_index[:, None])
    send_slot = owner * capacity + jnp.sum(earlier.astype(jnp.int32), axis=1)
    slot_ids = jnp.arange(data_groups * capacity, dtype=jnp.int32)
    placing = slot_ids[:, None] == send_slot[None, :]
    mp_count = lax.axis_size(MP_AXES)
    slot_share = PAGE_SLOTS // mp_count
    my_slots = lax.dynamic_slice_in_dim(cache_pages, part_index * slot_share, slot_share, 1)
    flat_rows = my_slots.reshape(pages_here, -1)
    mark_cols = 128
    marks_col = jnp.broadcast_to((target + 1).astype(jnp.bfloat16)[:, None], (pages_here, mark_cols))
    flat_marked = jnp.concatenate([flat_rows, marks_col], axis=1)
    packed = jnp.dot(placing.astype(jnp.bfloat16), flat_marked, preferred_element_type=jnp.float32)
    got_pages = lax.all_to_all(
        packed.astype(jnp.bfloat16).reshape(data_groups, capacity, -1),
        DP_AXES,
        split_axis=0,
        concat_axis=0,
        tiled=True,
    )
    got_flat = got_pages.reshape(data_groups * capacity, -1)
    flat_rows = got_flat[:, : flat_rows.shape[1]]
    got_marks = got_flat[:, flat_rows.shape[1]].astype(jnp.int32)
    choosing = (got_marks[None, :] == page_index[:, None] + 1).astype(jnp.bfloat16)
    pool_part = (
        jnp.dot(choosing, flat_rows, preferred_element_type=jnp.float32)
        .astype(jnp.bfloat16)
        .reshape(1, pages_here, slot_share, keyval_cols)
    )
    pool_parts = lax.all_gather(pool_part, MP_AXES, axis=0, tiled=True)
    kv_pool = jnp.transpose(pool_parts, (1, 0, 2, 3)).reshape(pages_here, PAGE_SLOTS, keyval_cols)
    heads_here = query_cols // head_dim
    shard_portion = QUERY_HEADS // KEYVALUE_HEADS
    kv_heads = key_column_width // head_dim
    global_heads = part_index * heads_here + jnp.arange(heads_here, dtype=jnp.int32)
    source_heads = global_heads // shard_portion
    query_grid = query_heads.reshape(row_count, heads_here, head_dim)
    key_page_grid = jnp.take(
        key_head_rows.reshape(row_count, kv_heads, head_dim), source_heads, axis=1
    )
    value_page_grid = jnp.take(
        value_head_rows.reshape(row_count, kv_heads, head_dim), source_heads, axis=1
    )
    scores = jnp.einsum(
        "qhd,khd->hqk", query_grid, key_page_grid, preferred_element_type=jnp.float32
    ) * head_dim ** (-0.5)
    scores = jnp.where(allowed[None, :, :], scores, -1e30)
    probs = softmax_rows(scores).astype(jnp.bfloat16)
    attended = jnp.einsum(
        "hqk,khd->qhd", probs, value_page_grid, preferred_element_type=jnp.float32
    )
    attended = attended.astype(jnp.bfloat16).reshape(row_count, query_cols)
    attn_part = to_relative(
        jnp.einsum("tr,cr->tc", attended, out_rows_t, preferred_element_type=jnp.float32),
        inverse=True,
        axes=("x",),
    )
    attn_total = lax.psum(attn_part.astype(jnp.bfloat16), MP_AXES).astype(jnp.float32)
    residual_all = inputs_wide + attn_total
    ffn_input = rms_rows(residual_all, ffn_gain).astype(jnp.bfloat16)
    kv_pool, ffn_input = lax.optimization_barrier((kv_pool, ffn_input))
    residual_own = lax.dynamic_slice_in_dim(residual_all, part_index * own_rows, own_rows, 0)
    gate = fold_rows(to_relative(ffn_input, axes=("x",)), gate_full)
    upward = fold_rows(to_relative(ffn_input), up_relative)
    hidden = (jax.nn.silu(gate) * upward).astype(jnp.bfloat16)
    down_part = to_relative(
        jnp.einsum("tf,cf->tc", hidden, down_relative_t, preferred_element_type=jnp.float32),
        inverse=True,
    )
    swap = [(0, 1), (1, 0)]
    high = lax.axis_index("yhi")
    half_rows = row_count // 2
    mine_half = lax.dynamic_slice_in_dim(down_part, high * half_rows, half_rows, 0)
    other_half = lax.dynamic_slice_in_dim(down_part, (1 - high) * half_rows, half_rows, 0)
    got_half = lax.ppermute(other_half.astype(jnp.bfloat16), "yhi", swap)
    half_sum = mine_half + got_half.astype(jnp.float32)
    core = lax.axis_index("core")
    mine_rows = lax.dynamic_slice_in_dim(half_sum, core * own_rows, own_rows, 0)
    other_rows = lax.dynamic_slice_in_dim(half_sum, (1 - core) * own_rows, own_rows, 0)
    got_rows = lax.ppermute(other_rows, "core", swap)
    layer_out = (residual_own + (mine_rows + got_rows)).astype(jnp.bfloat16)
    return (layer_out, kv_pool)


def solution(mesh):
    sizes = [mesh.shape["dp"] // (2 * 4), 2, 4, 2, mesh.shape["mp"] // 2]
    fine_mesh = Mesh(mesh.devices.reshape(sizes), DP_AXES + MP_AXES)
    rows = DP_AXES + MP_AXES
    return jax.shard_map(
        per_device,
        mesh=fine_mesh,
        in_specs=(
            P(rows, None),
            P(),
            P(DP_AXES, MP_AXES),
            P(rows, None),
            P(),
            P(),
            P(MP_AXES, DP_AXES),
            P(),
            P(None, DP_AXES, MP_AXES),
            P(MP_AXES, DP_AXES),
            P(DP_AXES, None),
            P(DP_AXES),
        ),
        out_specs=(P(rows, None), P(DP_AXES, None, None)),
        check_vma=False,
    )
```

```python
import jax
import jax.numpy as jnp
from jax import lax
from jax.sharding import Mesh, PartitionSpec as P

QUERY_HEADS = 20
KEYVALUE_HEADS = 5
PAGE_SLOTS = 16


EPSILON = 1e-06


def rms_rows(values, gain):
    scale = lax.rsqrt(jnp.mean(values * values, axis=-1, keepdims=True) + EPSILON)
    return values * scale * gain


def prompt_layout(lengths, row_count, head_dim):
    ends = jnp.cumsum(lengths)
    starts = ends - lengths
    row_index = jnp.arange(row_count, dtype=jnp.int32)
    segment = jnp.sum((row_index[:, None] >= ends[None, :]).astype(jnp.int32), axis=1)
    prompt_ids = jnp.arange(lengths.shape[0], dtype=jnp.int32)
    first_row = jnp.sum(
        jnp.where(segment[:, None] == prompt_ids[None, :], starts[None, :], 0), axis=1
    )
    position = row_index - first_row
    half_dim = head_dim // 2
    frequency = 10000.0 ** (-(jnp.arange(half_dim, dtype=jnp.float32) * (2.0 / head_dim)))
    angle = position.astype(jnp.float32)[:, None] * frequency[None, :]
    allowed = (segment[:, None] == segment[None, :]) & (row_index[None, :] <= row_index[:, None])
    return (allowed, jnp.cos(angle)[:, None, :], jnp.sin(angle)[:, None, :])


def rotate_heads(flat, gain, cosines, sines):
    row_count = flat.shape[0]
    head_dim = gain.shape[0]
    heads = rms_rows(flat.reshape(row_count, -1, head_dim), gain)
    half_dim = head_dim // 2
    first = heads[..., :half_dim]
    second = heads[..., half_dim:]
    turned = jnp.concatenate(
        [first * cosines - second * sines, second * cosines + first * sines], axis=-1
    )
    return turned.reshape(row_count, -1)


def softmax_rows(scores):
    peak = jnp.max(scores, axis=-1, keepdims=True)
    weights = jnp.exp(scores - peak)
    return weights / jnp.sum(weights, axis=-1, keepdims=True)


def fold_rows(left, piece):
    return jnp.dot(left, piece, preferred_element_type=jnp.float32)


DP_AXES = ("z", "ylo", "x")
MP_AXES = ("yhi", "core")


def gather_dp(flat):
    staged = ring_gather(flat, "x", lax.axis_size("x"), 0)
    for axis in ("ylo", "z"):
        staged = lax.all_gather(staged, axis, axis=0, tiled=True)
    return staged


def ring_gather(block, axis, count, at):
    forward_perm = [(i, (i + 1) % count) for i in range(count)]
    backward_perm = [(i, (i - 1) % count) for i in range(count)]
    chunks = {0: block}
    ahead = block
    behind = block
    for step in range(1, count // 2 + 1):
        if count == 2:
            chunks[1] = lax.ppermute(block, axis, forward_perm)
        elif step < count - step:
            ahead = lax.ppermute(ahead, axis, forward_perm)
            behind = lax.ppermute(behind, axis, backward_perm)
            chunks[count - step] = ahead
            chunks[step] = behind
        else:
            half = block.shape[-1] // 2
            first = lax.ppermute(ahead[..., :half], axis, forward_perm)
            second = lax.ppermute(behind[..., half:], axis, backward_perm)
            chunks[step] = jnp.concatenate([first, second], axis=-1)
    return jnp.stack([chunks[r] for r in range(count)], axis=at)


def to_relative(values, inverse=False, axes=DP_AXES):
    lead = values.shape[:-1]
    sizes = [lax.axis_size(axis) for axis in DP_AXES]
    grid = values.reshape(lead + tuple(sizes) + (-1,))
    for k, axis in enumerate(DP_AXES):
        if axis not in axes:
            continue
        shift = lax.axis_index(axis)
        grid = jnp.roll(grid, shift if inverse else -shift, axis=len(lead) + k)
    return grid.reshape(values.shape)


def per_device(
    tokens,
    attn_gain,
    query_weight,
    key_value_weight,
    query_gain,
    key_gain,
    out_weight,
    ffn_gain,
    gate_up_weight,
    down_weight,
    prompt_lengths,
    page_table,
):
    head_dim = query_gain.shape[0]
    data_groups = 1
    for axis in DP_AXES:
        data_groups *= lax.axis_size(axis)
    part_index = lax.axis_index(MP_AXES)
    own_rows = tokens.shape[0]
    group_tokens = lax.all_gather(tokens, MP_AXES, axis=0, tiled=True)
    row_count = group_tokens.shape[0]
    inputs_wide = group_tokens.astype(jnp.float32)
    normed = rms_rows(inputs_wide, attn_gain).astype(jnp.bfloat16)
    model_width = tokens.shape[1]
    query_cols = query_weight.shape[1]
    keyval_cols = key_value_weight.shape[1]
    kv_rows = lax.all_gather(key_value_weight, MP_AXES, axis=0, tiled=True)
    pieces = [
        query_weight,
        kv_rows,
        out_weight.T,
        gate_up_weight[0],
    ]
    widths = [piece.shape[1] for piece in pieces]
    sizes = [piece.size for piece in pieces]
    packed_weights = jnp.concatenate([piece.astype(jnp.bfloat16).reshape(-1) for piece in pieces])
    gathered = gather_dp(packed_weights)
    offsets = [0]
    for size in sizes:
        offsets.append(offsets[-1] + size)
    def piece_of(k):
        return gathered[:, offsets[k]:offsets[k + 1]].reshape(model_width, widths[k])
    query_full = piece_of(0)
    keyval_full = piece_of(1)
    out_rows_t = piece_of(2)
    gate_full = piece_of(3)
    ring_pieces = [gate_up_weight[1], down_weight.T]
    ring_size = ring_pieces[0].size
    ring_block = jnp.concatenate([piece.astype(jnp.bfloat16).reshape(-1) for piece in ring_pieces])
    for k, axis in enumerate(DP_AXES):
        ring_block = ring_gather(ring_block, axis, lax.axis_size(axis), k)
    ring_all = ring_block.reshape(data_groups, -1)
    ffn_width = gate_up_weight.shape[2]
    up_relative = ring_all[:, :ring_size].reshape(model_width, ffn_width)
    down_relative_t = ring_all[:, ring_size:].reshape(model_width, ffn_width)
    normed_x = to_relative(normed, axes=("x",))
    queries = fold_rows(normed_x, query_full)
    keyvals = fold_rows(normed_x, keyval_full)
    allowed, cosines, sines = prompt_layout(prompt_lengths[0], row_count, head_dim)
    key_column_width = keyval_cols // 2
    query_heads = rotate_heads(queries, query_gain, cosines, sines).astype(jnp.bfloat16)
    key_head_rows = rotate_heads(keyvals[:, :key_column_width], key_gain, cosines, sines).astype(
        jnp.bfloat16
    )
    value_head_rows = keyvals[:, key_column_width:].astype(jnp.bfloat16)
    cache_rows = jnp.concatenate([key_head_rows, value_head_rows], axis=1)
    pages_here = row_count // PAGE_SLOTS
    cache_pages = cache_rows.reshape(pages_here, PAGE_SLOTS, keyval_cols)
    capacity = pages_here // min(pages_here, data_groups)
    owner = page_table // pages_here
    target = page_table % pages_here
    page_index = jnp.arange(pages_here, dtype=jnp.int32)
    earlier = (owner[None, :] == owner[:, None]) & (page_index[None, :] < page_index[:, None])
    send_slot = owner * capacity + jnp.sum(earlier.astype(jnp.int32), axis=1)
    slot_ids = jnp.arange(data_groups * capacity, dtype=jnp.int32)
    placing = slot_ids[:, None] == send_slot[None, :]
    mp_count = lax.axis_size(MP_AXES)
    slot_share = PAGE_SLOTS // mp_count
    my_slots = lax.dynamic_slice_in_dim(cache_pages, part_index * slot_share, slot_share, 1)
    flat_rows = my_slots.reshape(pages_here, -1)
    mark_cols = 128
    marks_col = jnp.broadcast_to((target + 1).astype(jnp.bfloat16)[:, None], (pages_here, mark_cols))
    flat_marked = jnp.concatenate([flat_rows, marks_col], axis=1)
    packed = jnp.dot(placing.astype(jnp.bfloat16), flat_marked, preferred_element_type=jnp.float32)
    got_pages = lax.all_to_all(
        packed.astype(jnp.bfloat16).reshape(data_groups, capacity, -1),
        DP_AXES,
        split_axis=0,
        concat_axis=0,
        tiled=True,
    )
    got_flat = got_pages.reshape(data_groups * capacity, -1)
    flat_rows = got_flat[:, : flat_rows.shape[1]]
    got_marks = got_flat[:, flat_rows.shape[1]].astype(jnp.int32)
    choosing = (got_marks[None, :] == page_index[:, None] + 1).astype(jnp.bfloat16)
    pool_part = (
        jnp.dot(choosing, flat_rows, preferred_element_type=jnp.float32)
        .astype(jnp.bfloat16)
        .reshape(1, pages_here, slot_share, keyval_cols)
    )
    pair_swap = [(0, 1), (1, 0)]
    pool_pair = []
    for axis in ("core", "yhi"):
        other_part = lax.ppermute(pool_part, axis, pair_swap)
        low_first = lax.axis_index(axis) == 0
        pool_part = jnp.where(
            low_first,
            jnp.concatenate([pool_part, other_part], axis=0),
            jnp.concatenate([other_part, pool_part], axis=0),
        )
    pool_parts = pool_part
    kv_pool = jnp.transpose(pool_parts, (1, 0, 2, 3)).reshape(pages_here, PAGE_SLOTS, keyval_cols)
    heads_here = query_cols // head_dim
    shard_portion = QUERY_HEADS // KEYVALUE_HEADS
    kv_heads = key_column_width // head_dim
    global_heads = part_index * heads_here + jnp.arange(heads_here, dtype=jnp.int32)
    source_heads = global_heads // shard_portion
    query_grid = query_heads.reshape(row_count, heads_here, head_dim)
    key_page_grid = jnp.take(
        key_head_rows.reshape(row_count, kv_heads, head_dim), source_heads, axis=1
    )
    value_page_grid = jnp.take(
        value_head_rows.reshape(row_count, kv_heads, head_dim), source_heads, axis=1
    )
    scores = jnp.einsum(
        "qhd,khd->hqk", query_grid, key_page_grid, preferred_element_type=jnp.float32
    ) * head_dim ** (-0.5)
    scores = jnp.where(allowed[None, :, :], scores, -1e30)
    probs = softmax_rows(scores).astype(jnp.bfloat16)
    attended = jnp.einsum(
        "hqk,khd->qhd", probs, value_page_grid, preferred_element_type=jnp.float32
    )
    attended = attended.astype(jnp.bfloat16).reshape(row_count, query_cols)
    attn_part = to_relative(
        jnp.einsum("tr,cr->tc", attended, out_rows_t, preferred_element_type=jnp.float32),
        inverse=True,
        axes=("x",),
    )
    attn_total = lax.psum(attn_part.astype(jnp.bfloat16), MP_AXES).astype(jnp.float32)
    residual_all = inputs_wide + attn_total
    ffn_input = rms_rows(residual_all, ffn_gain).astype(jnp.bfloat16)
    residual_own = lax.dynamic_slice_in_dim(residual_all, part_index * own_rows, own_rows, 0)
    gate = fold_rows(to_relative(ffn_input, axes=("x",)), gate_full)
    upward = fold_rows(to_relative(ffn_input), up_relative)
    hidden = (jax.nn.silu(gate) * upward).astype(jnp.bfloat16)
    down_part = to_relative(
        jnp.einsum("tf,cf->tc", hidden, down_relative_t, preferred_element_type=jnp.float32),
        inverse=True,
    )
    swap = [(0, 1), (1, 0)]
    high = lax.axis_index("yhi")
    half_rows = row_count // 2
    mine_half = lax.dynamic_slice_in_dim(down_part, high * half_rows, half_rows, 0)
    other_half = lax.dynamic_slice_in_dim(down_part, (1 - high) * half_rows, half_rows, 0)
    got_half = lax.ppermute(other_half.astype(jnp.bfloat16), "yhi", swap)
    half_sum = mine_half + got_half.astype(jnp.float32)
    core = lax.axis_index("core")
    mine_rows = lax.dynamic_slice_in_dim(half_sum, core * own_rows, own_rows, 0)
    other_rows = lax.dynamic_slice_in_dim(half_sum, (1 - core) * own_rows, own_rows, 0)
    got_rows = lax.ppermute(other_rows, "core", swap)
    layer_out = (residual_own + (mine_rows + got_rows)).astype(jnp.bfloat16)
    return (layer_out, kv_pool)


def solution(mesh):
    sizes = [mesh.shape["dp"] // (2 * 4), 2, 4, 2, mesh.shape["mp"] // 2]
    fine_mesh = Mesh(mesh.devices.reshape(sizes), DP_AXES + MP_AXES)
    rows = DP_AXES + MP_AXES
    return jax.shard_map(
        per_device,
        mesh=fine_mesh,
        in_specs=(
            P(rows, None),
            P(),
            P(DP_AXES, MP_AXES),
            P(rows, None),
            P(),
            P(),
            P(MP_AXES, DP_AXES),
            P(),
            P(None, DP_AXES, MP_AXES),
            P(MP_AXES, DP_AXES),
            P(DP_AXES, None),
            P(DP_AXES),
        ),
        out_specs=(P(rows, None), P(DP_AXES, None, None)),
        check_vma=False,
    )
```
